256 devices in a mesh: section: 2 (over core), dp: 4 (over y), ctx: 32 (over x, z).
Axes of the slice: x: 4, y: 4, z: 8, core: 2. Of those that a mesh axis runs over, the one named last changes fastest.
Arguments:
- tokens: bfloat16 [8, 4096, 2048], P('dp', 'ctx'), parts along dimension 0, may hold values from -6 to 6
- w_qkv: bfloat16 [2, 2048, 4096], P('section', 'ctx'), may hold values from -0.125 to 0.125
- w_gate: bfloat16 [2, 2048, 32], P('section', 'ctx'), may hold values from -0.125 to 0.125
- norm_gain: float32 [2, 2048], P('section'), may hold values from 0.5 to 1.5
- conv_weight: bfloat16 [2, 4, 4096], P('section'), may hold values from -3 to 3
- decay_rate: float32 [2, 16], P('section'), may hold values from 2.4414063e-05 to 0.08
- dt_bias: float32 [2, 16], P('section'), may hold values from -1 to 1
- head_gain: float32 [2, 128], P('section'), may hold values from 0.1 to 1.9
Outputs:
- final_hidden: bfloat16 [8, 4096, 2048], P(('dp', 'section'), 'ctx'), parts along dimension 0
The draws below stay inside these ranges and needn't reach their ends.
There are 4 independent parts, one for each index of `dp`. The reference program is written for one: setup_inputs(seed, part) draws one part's arguments, and reference() takes and returns one part's arrays. A program takes and returns all parts, laid end to end along the dimension named above; an argument that names none is the same for every part. Nothing has to cross between parts.
All inputs are finite; a program needn't handle non-finite values.
Results may differ from the reference program's by a relative error of at most 0.022.
Values may be sent and summed in bfloat16 or wider, within the bound.
No kernel may reach another device: no remote copies, remote signals or barrier semaphores. Data moves between devices by JAX's collectives and lax.ppermute only.
A program may use at most 320 MiB of HBM per device.

```python
import math
import jax
import jax.numpy as jnp
from jax import lax

D = 2048
NK = 8
NV = 16
DK = 128
DV = 128
CONV = 4
BLOCK = 128
LAYERS = 2
MB = 2
QKV = 4096
TOKENS = 4096


def level_of(rng, shape, cuts, smallest, largest):
    factor_of, own = 1.0, jax.random.fold_in(rng, 6)
    for dim, shards_of in cuts:
        steps = jnp.exp(jax.random.uniform(jax.random.fold_in(own, dim), (shards_of,), jnp.float32, smallest / len(cuts), largest / len(cuts)))
        factor_of = factor_of * jnp.repeat(steps, shape[dim] // shards_of).reshape([-1 if axis == dim else 1 for axis in range(len(shape))])
    return factor_of


def bell_draw(stream_key, extent, width, reach, shards=(), kind=jnp.bfloat16):
    entries = width * jax.random.normal(stream_key, extent, jnp.float32)
    if shards:
        entries = entries * level_of(stream_key, extent, shards, -0.22, 0.18)
    return jnp.clip(entries, -reach, reach).astype(kind)


def setup_inputs(seed: int = 0, part: int = 0) -> dict:
    key_of = jax.random.split(jax.random.key(seed), 9)
    own_keys = jax.random.split(jax.random.fold_in(key_of[8], part), 9)
    tokens = bell_draw(own_keys[0], (MB, TOKENS, D), 1.0, 6.0, ((1, 32),))
    w_qkv = bell_draw(key_of[1], (LAYERS, D, QKV), D ** -0.5, 0.125, ((0, 2), (1, 32)))
    w_gate = bell_draw(key_of[2], (LAYERS, D, 2 * NV), D ** -0.5, 0.125, ((0, 2), (1, 32)))
    norm_gain = jnp.clip(1.0 + 0.1 * jax.random.normal(key_of[3], (LAYERS, D), jnp.float32), 0.5, 1.5)
    conv_weight = bell_draw(key_of[4], (LAYERS, CONV, QKV), CONV ** -0.5, 3.0, ((0, 2),))
    decay_rate = jnp.clip(jnp.exp(math.log(0.08) - 8.094623 * jax.random.uniform(key_of[5], (LAYERS, NV), jnp.float32) ** level_of(key_of[5], (LAYERS, NV), ((0, 2),), -0.2, 0.2)), 2.441406286379788e-05, 0.08)
    dt_bias = jnp.clip(jax.random.uniform(key_of[6], (LAYERS, NV), jnp.float32, -1.0, 1.0) * level_of(key_of[6], (LAYERS, NV), ((0, 2),), -0.4, 0.0), -1.0, 1.0)
    head_gain = jnp.clip(1.0 + 0.18 * jax.random.normal(key_of[7], (LAYERS, DV), jnp.float32), 0.1, 1.9)
    return dict(tokens=tokens, w_qkv=w_qkv, w_gate=w_gate, norm_gain=norm_gain, conv_weight=conv_weight, decay_rate=decay_rate, dt_bias=dt_bias, head_gain=head_gain)


PRECISE = lax.Precision.HIGHEST

def rms_rows(values, gain_row):
    inverse = lax.rsqrt(lax.optimization_barrier(jnp.mean(values * values, axis=-1, keepdims=True)) + 1e-06)
    return values * inverse * gain_row

def unit_rows(values):
    return values * lax.rsqrt(lax.optimization_barrier(jnp.sum(values * values, axis=-1, keepdims=True)) + 1e-06)

def conv_rows(padded, conv_taps):
    tap_count = conv_taps.shape[0]
    length = padded.shape[-2] - tap_count + 1
    running_sum = jnp.zeros(padded.shape[:-2] + (length, padded.shape[-1]), jnp.float32)
    for offset in range(tap_count):
        running_sum = running_sum + conv_taps[offset].astype(jnp.float32) * padded[..., offset:offset + length, :].astype(jnp.float32)
    return jax.nn.silu(running_sum).astype(jnp.bfloat16)

def head_inputs(mixed_rows, gate_raw, decay_rates, biases):
    row_count = mixed_rows.shape[0]
    features = mixed_rows.astype(jnp.float32)
    queries = unit_rows(features[:, :NK * DK].reshape(row_count, NK, DK)) * DK ** (-0.5)
    key_rows = unit_rows(features[:, NK * DK:2 * NK * DK].reshape(row_count, NK, DK))
    values = features[:, 2 * NK * DK:].reshape(row_count, NV, DV)
    queries = jnp.repeat(queries, NV // NK, axis=1)
    key_rows = jnp.repeat(key_rows, NV // NK, axis=1)
    gate_float = gate_raw.astype(jnp.float32)
    strength = jax.nn.sigmoid(gate_float[:, :NV])
    logdecay = -decay_rates * jax.nn.softplus(gate_float[:, NV:] + biases)
    return (queries, key_rows, values, strength, logdecay)

def block_parts(queries, key_rows, values, strength, logdecay):
    block_len = queries.shape[1]
    cumulative = jnp.swapaxes(jnp.cumsum(logdecay, axis=1), 1, 2)
    beta_heads = jnp.swapaxes(strength, 1, 2)
    query_heads = jnp.swapaxes(queries, 1, 2)
    key_heads = jnp.swapaxes(key_rows, 1, 2)
    value_heads = jnp.swapaxes(values, 1, 2)
    places = jnp.arange(block_len)
    lower_mask = places[:, None] >= places[None, :]
    strict_mask = places[:, None] > places[None, :]
    log_gap = cumulative[..., :, None] - cumulative[..., None, :]
    decay_ratio = jnp.where(lower_mask, jnp.exp(jnp.where(lower_mask, log_gap, 0.0)), 0.0)
    key_inner = jnp.einsum('nhid,nhjd->nhij', key_heads, key_heads, precision=PRECISE)
    system = jnp.where(strict_mask, beta_heads[..., :, None] * key_inner * decay_ratio, 0.0) + jnp.eye(block_len, dtype=queries.dtype)
    gamma_rows = jnp.exp(cumulative)
    right_side = jnp.concatenate([beta_heads[..., None] * value_heads, (beta_heads * gamma_rows)[..., None] * key_heads], axis=-1)
    solved = lax.linalg.triangular_solve(system, right_side, left_side=True, lower=True, unit_diagonal=True)
    fresh_rows = solved[..., :value_heads.shape[-1]]
    mixing = solved[..., value_heads.shape[-1]:]
    scores = jnp.einsum('nhid,nhjd->nhij', query_heads, key_heads, precision=PRECISE) * decay_ratio
    qgamma = gamma_rows[..., None] * query_heads
    key_tail = jnp.exp(cumulative[..., -1:] - cumulative)[..., None] * key_heads
    block_decay = gamma_rows[..., -1]
    return (fresh_rows, mixing, scores, qgamma, key_tail, block_decay)

def block_apply(state_now, block_items):
    fresh_rows, mixing, scores, qgamma, key_tail, block_decay = block_items
    update = fresh_rows - jnp.einsum('...cd,...de->...ce', mixing, state_now, precision=PRECISE)
    output = jnp.einsum('...cd,...de->...ce', qgamma, state_now, precision=PRECISE) + jnp.einsum('...ij,...je->...ie', scores, update, precision=PRECISE)
    state_next = block_decay[..., None, None] * state_now + jnp.einsum('...cd,...ce->...de', key_tail, update, precision=PRECISE)
    return (state_next, output)

def layer_apply(hidden, weight_qkv, weight_gate, gain_in, conv_taps, decay_rates, biases, gain_out):
    positions = hidden.shape[0]
    normed = rms_rows(hidden.astype(jnp.float32), gain_in).astype(jnp.bfloat16)
    features = jnp.dot(normed.astype(jnp.float32), weight_qkv.astype(jnp.float32), preferred_element_type=jnp.float32).astype(jnp.bfloat16)
    gate_raw = jnp.dot(normed.astype(jnp.float32), weight_gate.astype(jnp.float32), preferred_element_type=jnp.float32).astype(jnp.bfloat16)
    padded = jnp.concatenate([jnp.zeros((CONV - 1, features.shape[1]), jnp.bfloat16), features], axis=0)
    mixed_rows = conv_rows(padded, conv_taps)
    queries, key_rows, values, strength, logdecay = head_inputs(mixed_rows, gate_raw, decay_rates, biases)
    blocks = positions // BLOCK

    def advance(state_now, block_index):
        start_row = (block_index * BLOCK).astype(jnp.int32)
        pieces = [lax.dynamic_slice_in_dim(source, start_row, BLOCK, 0)[None] for source in (queries, key_rows, values, strength, logdecay)]
        parts = block_parts(pieces[0], pieces[1], pieces[2], pieces[3], pieces[4])
        parts = tuple((source[0] for source in parts))
        return block_apply(state_now, parts)
    _, outputs = lax.scan(advance, jnp.zeros((NV, DK, DV), jnp.float32), jnp.arange(blocks, dtype=jnp.int32))
    outputs = jnp.transpose(outputs, (0, 2, 1, 3)).reshape(positions, NV, DV)
    normed_out = rms_rows(outputs, gain_out).reshape(positions, NV * DV)
    return (hidden.astype(jnp.float32) + normed_out).astype(jnp.bfloat16)

def reference(tokens, w_qkv, w_gate, norm_gain, conv_weight, decay_rate, dt_bias, head_gain):
    finals = []
    for batch_index in range(MB):
        hidden = tokens[batch_index]
        for layer_index in range(LAYERS):
            hidden = layer_apply(hidden, w_qkv[layer_index], w_gate[layer_index], norm_gain[layer_index], conv_weight[layer_index], decay_rate[layer_index], dt_bias[layer_index], head_gain[layer_index])
        finals.append(hidden)
    return jnp.stack(finals)
```

```python
import jax
import jax.numpy as jnp
from jax import lax
from jax.sharding import PartitionSpec as P

NK = 8
NV = 16
DK = 128
DV = 128
CONV = 4
BLOCK = 128


PRECISE = lax.Precision.HIGHEST


def from_behind(value, axis, by):
    length = lax.axis_size(axis)
    pairs = [(i, i + by) for i in range(length) if 0 <= i + by < length]
    return lax.ppermute(value, axis, pairs)


def rms_rows(values, gain_row):
    inverse = lax.rsqrt(jnp.mean(values * values, axis=-1, keepdims=True) + 1e-06)
    return values * inverse * gain_row


def unit_rows(values):
    return values * lax.rsqrt(jnp.sum(values * values, axis=-1, keepdims=True) + 1e-06)


def conv_rows(padded, conv_taps):
    tap_count = conv_taps.shape[0]
    length = padded.shape[-2] - tap_count + 1
    running_sum = jnp.zeros(padded.shape[:-2] + (length, padded.shape[-1]), jnp.float32)
    for offset in range(tap_count):
        running_sum = running_sum + conv_taps[offset].astype(jnp.float32) * padded[
            ..., offset : offset + length, :
        ].astype(jnp.float32)
    return jax.nn.silu(running_sum).astype(jnp.bfloat16)


def head_inputs(mixed_rows, gate_raw, decay_rates, biases):
    row_count = mixed_rows.shape[0]
    features = mixed_rows.astype(jnp.float32)
    queries = unit_rows(features[:, : NK * DK].reshape(row_count, NK, DK)) * DK ** (-0.5)
    key_rows = unit_rows(features[:, NK * DK : 2 * NK * DK].reshape(row_count, NK, DK))
    values = features[:, 2 * NK * DK :].reshape(row_count, NV, DV)
    queries = jnp.repeat(queries, NV // NK, axis=1)
    key_rows = jnp.repeat(key_rows, NV // NK, axis=1)
    gate_float = gate_raw.astype(jnp.float32)
    strength = jax.nn.sigmoid(gate_float[:, :NV])
    logdecay = -decay_rates * jax.nn.softplus(gate_float[:, NV:] + biases)
    return (queries, key_rows, values, strength, logdecay)


def unit_lower_inverse(strict_part):
    size = strict_part.shape[-1]
    base = min(16, size)
    count = size // base
    lead = strict_part.shape[:-2]
    tiles = strict_part.reshape(lead + (count, base, count, base))
    diag_tiles = jnp.moveaxis(jnp.diagonal(tiles, axis1=-4, axis2=-2), -1, -3)
    inverse = jnp.broadcast_to(jnp.eye(base, dtype=strict_part.dtype), diag_tiles.shape)
    for row in range(1, base):
        new_row = -jnp.einsum(
            "...j,...jk->...k", diag_tiles[..., row, :], inverse, precision=PRECISE
        )
        new_row = new_row.at[..., row].add(1.0)
        inverse = inverse.at[..., row, :].set(new_row)
    width = base
    while width < size:
        pairs = size // (2 * width)
        tiles = strict_part.reshape(lead + (pairs, 2 * width, pairs, 2 * width))
        below = jnp.moveaxis(jnp.diagonal(tiles, axis1=-4, axis2=-2), -1, -3)[
            ..., width:, :width
        ]
        inverse = inverse.reshape(lead + (pairs, 2, width, width))
        upper = inverse[..., 0, :, :]
        lower = inverse[..., 1, :, :]
        corner = -jnp.einsum(
            "...ij,...jk->...ik",
            lower,
            jnp.einsum("...ij,...jk->...ik", below, upper, precision=PRECISE),
            precision=PRECISE,
        )
        zeros = jnp.zeros_like(upper)
        top = jnp.concatenate([upper, zeros], axis=-1)
        bottom = jnp.concatenate([corner, lower], axis=-1)
        inverse = jnp.concatenate([top, bottom], axis=-2)
        width *= 2
    return inverse.reshape(lead + (size, size))


def block_parts(queries, key_rows, values, strength, logdecay):
    block_len = queries.shape[1]
    cumulative = jnp.swapaxes(jnp.cumsum(logdecay, axis=1), 1, 2)
    beta_heads = jnp.swapaxes(strength, 1, 2)
    query_heads = jnp.swapaxes(queries, 1, 2)
    key_heads = jnp.swapaxes(key_rows, 1, 2)
    value_heads = jnp.swapaxes(values, 1, 2)
    places = jnp.arange(block_len)
    lower_mask = places[:, None] >= places[None, :]
    strict_mask = places[:, None] > places[None, :]
    log_gap = cumulative[..., :, None] - cumulative[..., None, :]
    decay_ratio = jnp.where(lower_mask, jnp.exp(jnp.where(lower_mask, log_gap, 0.0)), 0.0)
    key_inner = jnp.einsum("nhid,nhjd->nhij", key_heads, key_heads, precision=PRECISE)
    strict_part = jnp.where(strict_mask, beta_heads[..., :, None] * key_inner * decay_ratio, 0.0)
    gamma_rows = jnp.exp(cumulative)
    right_side = jnp.concatenate(
        [beta_heads[..., None] * value_heads, (beta_heads * gamma_rows)[..., None] * key_heads],
        axis=-1,
    )
    solved = jnp.einsum(
        "...ij,...jk->...ik", unit_lower_inverse(strict_part), right_side, precision=PRECISE
    )
    fresh_rows = solved[..., : value_heads.shape[-1]]
    mixing = solved[..., value_heads.shape[-1] :]
    scores = jnp.einsum("nhid,nhjd->nhij", query_heads, key_heads, precision=PRECISE) * decay_ratio
    qgamma = gamma_rows[..., None] * query_heads
    key_tail = jnp.exp(cumulative[..., -1:] - cumulative)[..., None] * key_heads
    block_decay = gamma_rows[..., -1]
    return (fresh_rows, mixing, scores, qgamma, key_tail, block_decay)


def block_apply(state_now, block_items):
    fresh_rows, mixing, scores, qgamma, key_tail, block_decay = block_items
    update = fresh_rows - jnp.einsum("...cd,...de->...ce", mixing, state_now, precision=PRECISE)
    output = jnp.einsum("...cd,...de->...ce", qgamma, state_now, precision=PRECISE) + jnp.einsum(
        "...ij,...je->...ie", scores, update, precision=PRECISE
    )
    state_next = block_decay[..., None, None] * state_now + jnp.einsum(
        "...cd,...ce->...de", key_tail, update, precision=PRECISE
    )
    return (state_next, output)


def chain_product(left_map, right_map):
    return jnp.einsum("...ij,...jk->...ik", left_map, right_map, precision=PRECISE)


def local(tokens, w_qkv, w_gate, norm_gain, conv_weight, decay_rate, dt_bias, head_gain):
    section = lax.axis_index("section")
    layer_count = lax.axis_size("section")

    def every_layer(value):
        return lax.all_gather(value[0], "section", axis=0, tiled=False)

    all_qkv = every_layer(w_qkv)
    all_gate = every_layer(w_gate)
    all_gain_in = every_layer(norm_gain)
    all_taps = every_layer(conv_weight)
    all_rates = every_layer(decay_rate)
    all_biases = every_layer(dt_bias)
    all_gain_out = every_layer(head_gain)
    hidden = lax.dynamic_slice_in_dim(tokens, section, 1, axis=0)
    for layer_index in range(layer_count):
        full_qkv = lax.all_gather(all_qkv[layer_index], "ctx", axis=0, tiled=True)
        full_gate = lax.all_gather(all_gate[layer_index], "ctx", axis=0, tiled=True)
        hidden = layer_apply(
            hidden,
            full_qkv,
            full_gate,
            all_gain_in[layer_index],
            all_taps[layer_index],
            all_rates[layer_index],
            all_biases[layer_index],
            all_gain_out[layer_index],
        )
    return hidden


def layer_apply(section_input, full_qkv, full_gate, gain_in, conv_taps, decay_rates, biases, gain_out):
    groups, positions, model_width = section_input.shape
    blocks = positions // BLOCK
    layer_normed = (
        rms_rows(section_input.astype(jnp.float32), gain_in)
        .astype(jnp.bfloat16)
        .reshape(groups * positions, model_width)
    )
    proj_qkv = jnp.dot(layer_normed, full_qkv, preferred_element_type=jnp.float32)
    proj_gate = jnp.dot(layer_normed, full_gate, preferred_element_type=jnp.float32)
    features = proj_qkv.astype(jnp.bfloat16).reshape(groups, positions, proj_qkv.shape[1])
    gate_raw = proj_gate.astype(jnp.bfloat16)
    previous_rows = from_behind(features[:, positions - (CONV - 1) :], "ctx", 1)
    mixed_rows = conv_rows(jnp.concatenate([previous_rows, features], axis=1), conv_taps)
    queries, key_rows, values, strength, logdecay = head_inputs(
        mixed_rows.reshape(groups * positions, mixed_rows.shape[2]),
        gate_raw,
        decay_rates,
        biases,
    )
    count_blocks = groups * blocks
    parts = block_parts(
        queries.reshape(count_blocks, BLOCK, NV, DK),
        key_rows.reshape(count_blocks, BLOCK, NV, DK),
        values.reshape(count_blocks, BLOCK, NV, DV),
        strength.reshape(count_blocks, BLOCK, NV),
        logdecay.reshape(count_blocks, BLOCK, NV),
    )
    parts = tuple(
        (
            jnp.moveaxis(source.reshape((groups, blocks) + source.shape[1:]), 1, 0)
            for source in parts
        )
    )
    fresh_rows, mixing, scores, qgamma, key_tail, block_decay = parts
    identity = jnp.broadcast_to(jnp.eye(DK, dtype=jnp.float32), (groups, NV, DK, DK))
    no_state = jnp.zeros((groups, NV, DK, DV), jnp.float32)
    step_maps = block_decay[..., None, None] * identity - jnp.einsum(
        "...cd,...cf->...df", key_tail, mixing, precision=PRECISE
    )
    step_biases = jnp.einsum("...cd,...ce->...de", key_tail, fresh_rows, precision=PRECISE)

    def compose(running, block_items):
        map_now, bias_now = running
        step_map, step_bias = block_items
        return (
            (chain_product(step_map, map_now), chain_product(step_map, bias_now) + step_bias),
            None,
        )

    (local_map, local_bias), _ = lax.scan(
        compose, (identity, no_state), (step_maps, step_biases)
    )
    ctx_count = lax.axis_size("ctx")
    column_parts = max(1, ctx_count // NV)
    item_count = NV * column_parts
    part_width = DV // column_parts
    sent_maps = jnp.repeat(local_map, column_parts, axis=1)[None]
    sent_bias = jnp.moveaxis(local_bias.reshape(groups, NV, DK, column_parts, part_width), 3, 2)
    sent_bias = sent_bias.reshape(groups, item_count, DK, part_width)[None]
    got_maps = lax.all_to_all(sent_maps, "ctx", split_axis=2, concat_axis=0, tiled=True)
    got_bias = lax.all_to_all(sent_bias, "ctx", split_axis=2, concat_axis=0, tiled=True)

    def chain_step(state_now, incoming):
        return (chain_product(incoming[0], state_now) + incoming[1], state_now)

    _, entering_parts = lax.scan(
        chain_step, jnp.zeros(got_bias.shape[1:], jnp.float32), (got_maps, got_bias)
    )
    returned_states = lax.all_to_all(
        entering_parts, "ctx", split_axis=0, concat_axis=2, tiled=True
    )
    entering = returned_states[0].reshape(groups, NV, column_parts, DK, part_width)
    entering = jnp.moveaxis(entering, 2, 3).reshape(groups, NV, DK, DV)
    _, outputs = lax.scan(block_apply, entering, parts)
    outputs = jnp.transpose(outputs, (1, 0, 3, 2, 4)).reshape(groups, positions, NV, DV)
    normed_out = rms_rows(outputs, gain_out).reshape(groups, positions, NV * DV)
    outcome = (section_input.astype(jnp.float32) + normed_out).astype(jnp.bfloat16)
    return outcome


def solution(mesh):
    return jax.shard_map(
        local,
        mesh=mesh,
        in_specs=(
            P("dp", "ctx", None),
            P("section", "ctx", None),
            P("section", "ctx", None),
            P("section", None),
            P("section", None, None),
            P("section", None),
            P("section", None),
            P("section", None),
        ),
        out_specs=P(("dp", "section"), "ctx", None),
        check_vma=False,
    )
```

```python
import jax
import jax.numpy as jnp
from jax import lax
from jax.sharding import PartitionSpec as P

NK = 8
NV = 16
DK = 128
DV = 128
CONV = 4
BLOCK = 128


PRECISE = lax.Precision.HIGHEST


def from_behind(value, axis, by):
    length = lax.axis_size(axis)
    pairs = [(i, i + by) for i in range(length) if 0 <= i + by < length]
    return lax.ppermute(value, axis, pairs)


def rms_rows(values, gain_row):
    inverse = lax.rsqrt(jnp.mean(values * values, axis=-1, keepdims=True) + 1e-06)
    return values * inverse * gain_row


def unit_rows(values):
    return values * lax.rsqrt(jnp.sum(values * values, axis=-1, keepdims=True) + 1e-06)


def conv_rows(padded, conv_taps):
    tap_count = conv_taps.shape[0]
    length = padded.shape[-2] - tap_count + 1
    running_sum = jnp.zeros(padded.shape[:-2] + (length, padded.shape[-1]), jnp.float32)
    for offset in range(tap_count):
        running_sum = running_sum + conv_taps[offset].astype(jnp.float32) * padded[
            ..., offset : offset + length, :
        ].astype(jnp.float32)
    return jax.nn.silu(running_sum).astype(jnp.bfloat16)


def head_inputs(mixed_rows, gate_raw, decay_rates, biases):
    row_count = mixed_rows.shape[0]
    features = mixed_rows.astype(jnp.float32)
    queries = unit_rows(features[:, : NK * DK].reshape(row_count, NK, DK)) * DK ** (-0.5)
    key_rows = unit_rows(features[:, NK * DK : 2 * NK * DK].reshape(row_count, NK, DK))
    values = features[:, 2 * NK * DK :].reshape(row_count, NV, DV)
    queries = jnp.repeat(queries, NV // NK, axis=1)
    key_rows = jnp.repeat(key_rows, NV // NK, axis=1)
    gate_float = gate_raw.astype(jnp.float32)
    strength = jax.nn.sigmoid(gate_float[:, :NV])
    logdecay = -decay_rates * jax.nn.softplus(gate_float[:, NV:] + biases)
    return (queries, key_rows, values, strength, logdecay)


def unit_lower_inverse(strict_part):
    size = strict_part.shape[-1]
    base = min(8, size)
    count = size // base
    lead = strict_part.shape[:-2]
    tiles = strict_part.reshape(lead + (count, base, count, base))
    diag_tiles = jnp.moveaxis(jnp.diagonal(tiles, axis1=-4, axis2=-2), -1, -3)
    identity = jnp.eye(base, dtype=strict_part.dtype)
    inverse = identity - diag_tiles
    power = diag_tiles
    reach = 2
    while reach < base:
        power = jnp.einsum("...ij,...jk->...ik", power, power, precision=PRECISE)
        inverse = inverse + jnp.einsum("...ij,...jk->...ik", inverse, power, precision=PRECISE)
        reach *= 2
    width = base
    while width < size:
        pairs = size // (2 * width)
        tiles = strict_part.reshape(lead + (pairs, 2 * width, pairs, 2 * width))
        below = jnp.moveaxis(jnp.diagonal(tiles, axis1=-4, axis2=-2), -1, -3)[
            ..., width:, :width
        ]
        inverse = inverse.reshape(lead + (pairs, 2, width, width))
        upper = inverse[..., 0, :, :]
        lower = inverse[..., 1, :, :]
        corner = -jnp.einsum(
            "...ij,...jk->...ik",
            lower,
            jnp.einsum("...ij,...jk->...ik", below, upper, precision=PRECISE),
            precision=PRECISE,
        )
        zeros = jnp.zeros_like(upper)
        top = jnp.concatenate([upper, zeros], axis=-1)
        bottom = jnp.concatenate([corner, lower], axis=-1)
        inverse = jnp.concatenate([top, bottom], axis=-2)
        width *= 2
    return inverse.reshape(lead + (size, size))


def block_parts(queries, key_rows, values, strength, logdecay):
    block_len = queries.shape[1]
    cumulative = jnp.swapaxes(jnp.cumsum(logdecay, axis=1), 1, 2)
    beta_heads = jnp.swapaxes(strength, 1, 2)
    query_heads = jnp.swapaxes(queries, 1, 2)
    key_heads = jnp.swapaxes(key_rows, 1, 2)
    value_heads = jnp.swapaxes(values, 1, 2)
    places = jnp.arange(block_len)
    lower_mask = places[:, None] >= places[None, :]
    strict_mask = places[:, None] > places[None, :]
    log_gap = cumulative[..., :, None] - cumulative[..., None, :]
    decay_ratio = jnp.where(lower_mask, jnp.exp(jnp.where(lower_mask, log_gap, 0.0)), 0.0)
    key_inner = jnp.einsum("nhid,nhjd->nhij", key_heads, key_heads, precision=PRECISE)
    strict_part = jnp.where(strict_mask, beta_heads[..., :, None] * key_inner * decay_ratio, 0.0)
    gamma_rows = jnp.exp(cumulative)
    right_side = jnp.concatenate(
        [beta_heads[..., None] * value_heads, (beta_heads * gamma_rows)[..., None] * key_heads],
        axis=-1,
    )
    solved = jnp.einsum(
        "...ij,...jk->...ik", unit_lower_inverse(strict_part), right_side, precision=PRECISE
    )
    fresh_rows = solved[..., : value_heads.shape[-1]]
    mixing = solved[..., value_heads.shape[-1] :]
    scores = jnp.einsum("nhid,nhjd->nhij", query_heads, key_heads, precision=PRECISE) * decay_ratio
    qgamma = gamma_rows[..., None] * query_heads
    key_tail = jnp.exp(cumulative[..., -1:] - cumulative)[..., None] * key_heads
    block_decay = gamma_rows[..., -1]
    return (fresh_rows, mixing, scores, qgamma, key_tail, block_decay)


def block_apply(state_now, block_items):
    fresh_rows, mixing, scores, qgamma, key_tail, block_decay = block_items
    update = fresh_rows - jnp.einsum("...cd,...de->...ce", mixing, state_now, precision=PRECISE)
    output = jnp.einsum("...cd,...de->...ce", qgamma, state_now, precision=PRECISE) + jnp.einsum(
        "...ij,...je->...ie", scores, update, precision=PRECISE
    )
    state_next = block_decay[..., None, None] * state_now + jnp.einsum(
        "...cd,...ce->...de", key_tail, update, precision=PRECISE
    )
    return (state_next, output)


def chain_product(left_map, right_map):
    return jnp.einsum("...ij,...jk->...ik", left_map, right_map, precision=PRECISE)


def local(tokens, w_qkv, w_gate, norm_gain, conv_weight, decay_rate, dt_bias, head_gain):
    section = lax.axis_index("section")
    layer_count = lax.axis_size("section")

    def every_layer(value):
        held = [value]
        for offset in range(1, layer_count):
            pairs = [(i, (i + offset) % layer_count) for i in range(layer_count)]
            held.append(lax.ppermute(value, "section", pairs))
        layers = []
        for layer_index in range(layer_count):
            owner_offset = (section - layer_index) % layer_count
            chosen = held[0]
            for offset in range(1, layer_count):
                chosen = jnp.where(owner_offset == offset, held[offset], chosen)
            layers.append(chosen[0])
        return layers

    all_qkv = every_layer(w_qkv)
    all_gate = every_layer(w_gate)
    all_gain_in = every_layer(norm_gain)
    all_taps = every_layer(conv_weight)
    all_rates = every_layer(decay_rate)
    all_biases = every_layer(dt_bias)
    all_gain_out = every_layer(head_gain)
    hidden = lax.dynamic_slice_in_dim(tokens, section, 1, axis=0)
    for layer_index in range(layer_count):
        full_qkv = lax.all_gather(all_qkv[layer_index], "ctx", axis=0, tiled=True)
        full_gate = lax.all_gather(all_gate[layer_index], "ctx", axis=0, tiled=True)
        hidden = layer_apply(
            hidden,
            full_qkv,
            full_gate,
            all_gain_in[layer_index],
            all_taps[layer_index],
            all_rates[layer_index],
            all_biases[layer_index],
            all_gain_out[layer_index],
        )
    return hidden


def layer_apply(section_input, full_qkv, full_gate, gain_in, conv_taps, decay_rates, biases, gain_out):
    groups, positions, model_width = section_input.shape
    blocks = positions // BLOCK
    layer_normed = (
        rms_rows(section_input.astype(jnp.float32), gain_in)
        .astype(jnp.bfloat16)
        .reshape(groups * positions, model_width)
    )
    proj_qkv = jnp.dot(layer_normed, full_qkv, preferred_element_type=jnp.float32)
    proj_gate = jnp.dot(layer_normed, full_gate, preferred_element_type=jnp.float32)
    features = proj_qkv.astype(jnp.bfloat16).reshape(groups, positions, proj_qkv.shape[1])
    gate_raw = proj_gate.astype(jnp.bfloat16)
    previous_rows = from_behind(features[:, positions - (CONV - 1) :], "ctx", 1)
    mixed_rows = conv_rows(jnp.concatenate([previous_rows, features], axis=1), conv_taps)
    queries, key_rows, values, strength, logdecay = head_inputs(
        mixed_rows.reshape(groups * positions, mixed_rows.shape[2]),
        gate_raw,
        decay_rates,
        biases,
    )
    count_blocks = groups * blocks
    parts = block_parts(
        queries.reshape(count_blocks, BLOCK, NV, DK),
        key_rows.reshape(count_blocks, BLOCK, NV, DK),
        values.reshape(count_blocks, BLOCK, NV, DV),
        strength.reshape(count_blocks, BLOCK, NV),
        logdecay.reshape(count_blocks, BLOCK, NV),
    )
    parts = tuple(
        (
            jnp.moveaxis(source.reshape((groups, blocks) + source.shape[1:]), 1, 0)
            for source in parts
        )
    )
    fresh_rows, mixing, scores, qgamma, key_tail, block_decay = parts
    identity = jnp.broadcast_to(jnp.eye(DK, dtype=jnp.float32), (groups, NV, DK, DK))
    no_state = jnp.zeros((groups, NV, DK, DV), jnp.float32)
    step_maps = block_decay[..., None, None] * identity - jnp.einsum(
        "...cd,...cf->...df", key_tail, mixing, precision=PRECISE
    )
    step_biases = jnp.einsum("...cd,...ce->...de", key_tail, fresh_rows, precision=PRECISE)

    def compose(running, block_items):
        map_now, bias_now = running
        step_map, step_bias = block_items
        return (
            (chain_product(step_map, map_now), chain_product(step_map, bias_now) + step_bias),
            None,
        )

    (local_map, local_bias), _ = lax.scan(
        compose, (identity, no_state), (step_maps, step_biases)
    )
    ctx_count = lax.axis_size("ctx")
    column_parts = max(1, ctx_count // NV)
    item_count = NV * column_parts
    part_width = DV // column_parts
    sent_maps = jnp.repeat(local_map, column_parts, axis=1)[None]
    sent_bias = jnp.moveaxis(local_bias.reshape(groups, NV, DK, column_parts, part_width), 3, 2)
    sent_bias = sent_bias.reshape(groups, item_count, DK, part_width)[None]
    got_maps = lax.all_to_all(sent_maps, "ctx", split_axis=2, concat_axis=0, tiled=True)
    got_bias = lax.all_to_all(sent_bias, "ctx", split_axis=2, concat_axis=0, tiled=True)

    def chain_step(state_now, incoming):
        return (chain_product(incoming[0], state_now) + incoming[1], state_now)

    _, entering_parts = lax.scan(
        chain_step, jnp.zeros(got_bias.shape[1:], jnp.float32), (got_maps, got_bias)
    )
    returned_states = lax.all_to_all(
        entering_parts, "ctx", split_axis=0, concat_axis=2, tiled=True
    )
    entering = returned_states[0].reshape(groups, NV, column_parts, DK, part_width)
    entering = jnp.moveaxis(entering, 2, 3).reshape(groups, NV, DK, DV)
    _, outputs = lax.scan(block_apply, entering, parts)
    outputs = jnp.transpose(outputs, (1, 0, 3, 2, 4)).reshape(groups, positions, NV, DV)
    normed_out = rms_rows(outputs, gain_out).reshape(groups, positions, NV * DV)
    outcome = (section_input.astype(jnp.float32) + normed_out).astype(jnp.bfloat16)
    return outcome


def solution(mesh):
    return jax.shard_map(
        local,
        mesh=mesh,
        in_specs=(
            P("dp", "ctx", None),
            P("section", "ctx", None),
            P("section", "ctx", None),
            P("section", None),
            P("section", None, None),
            P("section", None),
            P("section", None),
            P("section", None),
        ),
        out_specs=P(("dp", "section"), "ctx", None),
        check_vma=False,
    )
```

```python
import jax
import jax.numpy as jnp
from jax import lax
from jax.sharding import PartitionSpec as P

NK = 8
NV = 16
DK = 128
DV = 128
CONV = 4
BLOCK = 128


PRECISE = lax.Precision.HIGHEST


def from_behind(value, axis, by):
    length = lax.axis_size(axis)
    pairs = [(i, i + by) for i in range(length) if 0 <= i + by < length]
    return lax.ppermute(value, axis, pairs)


def rms_rows(values, gain_row):
    inverse = lax.rsqrt(jnp.mean(values * values, axis=-1, keepdims=True) + 1e-06)
    return values * inverse * gain_row


def unit_rows(values):
    return values * lax.rsqrt(jnp.sum(values * values, axis=-1, keepdims=True) + 1e-06)


def conv_rows(padded, conv_taps):
    tap_count = conv_taps.shape[0]
    length = padded.shape[-2] - tap_count + 1
    running_sum = jnp.zeros(padded.shape[:-2] + (length, padded.shape[-1]), jnp.float32)
    for offset in range(tap_count):
        running_sum = running_sum + conv_taps[offset].astype(jnp.float32) * padded[
            ..., offset : offset + length, :
        ].astype(jnp.float32)
    return jax.nn.silu(running_sum).astype(jnp.bfloat16)


def head_inputs(mixed_rows, gate_raw, decay_rates, biases):
    row_count = mixed_rows.shape[0]
    features = mixed_rows.astype(jnp.float32)
    queries = unit_rows(features[:, : NK * DK].reshape(row_count, NK, DK)) * DK ** (-0.5)
    key_rows = unit_rows(features[:, NK * DK : 2 * NK * DK].reshape(row_count, NK, DK))
    values = features[:, 2 * NK * DK :].reshape(row_count, NV, DV)
    queries = jnp.repeat(queries, NV // NK, axis=1)
    key_rows = jnp.repeat(key_rows, NV // NK, axis=1)
    gate_float = gate_raw.astype(jnp.float32)
    strength = jax.nn.sigmoid(gate_float[:, :NV])
    logdecay = -decay_rates * jax.nn.softplus(gate_float[:, NV:] + biases)
    return (queries, key_rows, values, strength, logdecay)


def unit_lower_inverse(strict_part):
    size = strict_part.shape[-1]
    base = min(8, size)
    count = size // base
    lead = strict_part.shape[:-2]
    tiles = strict_part.reshape(lead + (count, base, count, base))
    diag_tiles = jnp.moveaxis(jnp.diagonal(tiles, axis1=-4, axis2=-2), -1, -3)
    identity = jnp.eye(base, dtype=strict_part.dtype)
    inverse = identity - diag_tiles
    power = diag_tiles
    reach = 2
    while reach < base:
        power = jnp.einsum("...ij,...jk->...ik", power, power, precision=PRECISE)
        inverse = inverse + jnp.einsum("...ij,...jk->...ik", inverse, power, precision=PRECISE)
        reach *= 2
    width = base
    while width < size:
        pairs = size // (2 * width)
        tiles = strict_part.reshape(lead + (pairs, 2 * width, pairs, 2 * width))
        below = jnp.moveaxis(jnp.diagonal(tiles, axis1=-4, axis2=-2), -1, -3)[
            ..., width:, :width
        ]
        inverse = inverse.reshape(lead + (pairs, 2, width, width))
        upper = inverse[..., 0, :, :]
        lower = inverse[..., 1, :, :]
        corner = -jnp.einsum(
            "...ij,...jk->...ik",
            lower,
            jnp.einsum("...ij,...jk->...ik", below, upper, precision=PRECISE),
            precision=PRECISE,
        )
        zeros = jnp.zeros_like(upper)
        top = jnp.concatenate([upper, zeros], axis=-1)
        bottom = jnp.concatenate([corner, lower], axis=-1)
        inverse = jnp.concatenate([top, bottom], axis=-2)
        width *= 2
    return inverse.reshape(lead + (size, size))


def block_parts(queries, key_rows, values, strength, logdecay):
    block_len = queries.shape[1]
    cumulative = jnp.swapaxes(jnp.cumsum(logdecay, axis=1), 1, 2)
    beta_heads = jnp.swapaxes(strength, 1, 2)
    query_heads = jnp.swapaxes(queries, 1, 2)
    key_heads = jnp.swapaxes(key_rows, 1, 2)
    value_heads = jnp.swapaxes(values, 1, 2)
    places = jnp.arange(block_len)
    lower_mask = places[:, None] >= places[None, :]
    strict_mask = places[:, None] > places[None, :]
    log_gap = cumulative[..., :, None] - cumulative[..., None, :]
    decay_ratio = jnp.where(lower_mask, jnp.exp(jnp.where(lower_mask, log_gap, 0.0)), 0.0)
    key_inner = jnp.einsum("nhid,nhjd->nhij", key_heads, key_heads, precision=PRECISE)
    strict_part = jnp.where(strict_mask, beta_heads[..., :, None] * key_inner * decay_ratio, 0.0)
    gamma_rows = jnp.exp(cumulative)
    right_side = jnp.concatenate(
        [beta_heads[..., None] * value_heads, (beta_heads * gamma_rows)[..., None] * key_heads],
        axis=-1,
    )
    solved = jnp.einsum(
        "...ij,...jk->...ik", unit_lower_inverse(strict_part), right_side, precision=PRECISE
    )
    fresh_rows = solved[..., : value_heads.shape[-1]]
    mixing = solved[..., value_heads.shape[-1] :]
    scores = jnp.einsum("nhid,nhjd->nhij", query_heads, key_heads, precision=PRECISE) * decay_ratio
    qgamma = gamma_rows[..., None] * query_heads
    key_tail = jnp.exp(cumulative[..., -1:] - cumulative)[..., None] * key_heads
    block_decay = gamma_rows[..., -1]
    return (fresh_rows, mixing, scores, qgamma, key_tail, block_decay)


def block_apply(state_now, block_items):
    fresh_rows, mixing, scores, qgamma, key_tail, block_decay = block_items
    update = fresh_rows - jnp.einsum("...cd,...de->...ce", mixing, state_now, precision=PRECISE)
    output = jnp.einsum("...cd,...de->...ce", qgamma, state_now, precision=PRECISE) + jnp.einsum(
        "...ij,...je->...ie", scores, update, precision=PRECISE
    )
    state_next = block_decay[..., None, None] * state_now + jnp.einsum(
        "...cd,...ce->...de", key_tail, update, precision=PRECISE
    )
    return (state_next, output)


def chain_product(left_map, right_map):
    return jnp.einsum("...ij,...jk->...ik", left_map, right_map, precision=PRECISE)


def local(tokens, w_qkv, w_gate, norm_gain, conv_weight, decay_rate, dt_bias, head_gain):
    section = lax.axis_index("section")
    layer_count = lax.axis_size("section")

    def every_layer(value):
        held = [value]
        for offset in range(1, layer_count):
            pairs = [(i, (i + offset) % layer_count) for i in range(layer_count)]
            held.append(lax.ppermute(value, "section", pairs))
        layers = []
        for layer_index in range(layer_count):
            owner_offset = (section - layer_index) % layer_count
            chosen = held[0]
            for offset in range(1, layer_count):
                chosen = jnp.where(owner_offset == offset, held[offset], chosen)
            layers.append(chosen[0])
        return layers

    all_weights = every_layer(jnp.concatenate([w_qkv, w_gate], axis=2))
    all_gain_in = every_layer(norm_gain)
    all_taps = every_layer(conv_weight)
    all_rates = every_layer(decay_rate)
    all_biases = every_layer(dt_bias)
    all_gain_out = every_layer(head_gain)
    hidden = lax.dynamic_slice_in_dim(tokens, section, 1, axis=0)
    for layer_index in range(layer_count):
        full_weights = lax.all_gather(all_weights[layer_index], "ctx", axis=0, tiled=True)
        hidden = layer_apply(
            hidden,
            full_weights,
            all_gain_in[layer_index],
            all_taps[layer_index],
            all_rates[layer_index],
            all_biases[layer_index],
            all_gain_out[layer_index],
        )
    return hidden


def layer_apply(section_input, full_weights, gain_in, conv_taps, decay_rates, biases, gain_out):
    groups, positions, model_width = section_input.shape
    blocks = positions // BLOCK
    layer_normed = (
        rms_rows(section_input.astype(jnp.float32), gain_in)
        .astype(jnp.bfloat16)
        .reshape(groups * positions, model_width)
    )
    projected = jnp.dot(layer_normed, full_weights, preferred_element_type=jnp.float32)
    qkv_width = full_weights.shape[1] - 2 * NV
    proj_qkv = projected[:, :qkv_width]
    proj_gate = projected[:, qkv_width:]
    features = proj_qkv.astype(jnp.bfloat16).reshape(groups, positions, proj_qkv.shape[1])
    gate_raw = proj_gate.astype(jnp.bfloat16)
    previous_rows = from_behind(features[:, positions - (CONV - 1) :], "ctx", 1)
    mixed_rows = conv_rows(jnp.concatenate([previous_rows, features], axis=1), conv_taps)
    queries, key_rows, values, strength, logdecay = head_inputs(
        mixed_rows.reshape(groups * positions, mixed_rows.shape[2]),
        gate_raw,
        decay_rates,
        biases,
    )
    count_blocks = groups * blocks
    parts = block_parts(
        queries.reshape(count_blocks, BLOCK, NV, DK),
        key_rows.reshape(count_blocks, BLOCK, NV, DK),
        values.reshape(count_blocks, BLOCK, NV, DV),
        strength.reshape(count_blocks, BLOCK, NV),
        logdecay.reshape(count_blocks, BLOCK, NV),
    )
    parts = tuple(
        (
            jnp.moveaxis(source.reshape((groups, blocks) + source.shape[1:]), 1, 0)
            for source in parts
        )
    )
    fresh_rows, mixing, scores, qgamma, key_tail, block_decay = parts
    identity = jnp.broadcast_to(jnp.eye(DK, dtype=jnp.float32), (groups, NV, DK, DK))
    no_state = jnp.zeros((groups, NV, DK, DV), jnp.float32)
    step_maps = block_decay[..., None, None] * identity - jnp.einsum(
        "...cd,...cf->...df", key_tail, mixing, precision=PRECISE
    )
    step_biases = jnp.einsum("...cd,...ce->...de", key_tail, fresh_rows, precision=PRECISE)

    def compose(running, block_items):
        map_now, bias_now = running
        step_map, step_bias = block_items
        return (
            (chain_product(step_map, map_now), chain_product(step_map, bias_now) + step_bias),
            None,
        )

    (local_map, local_bias), _ = lax.scan(
        compose, (identity, no_state), (step_maps, step_biases)
    )
    ctx_count = lax.axis_size("ctx")
    column_parts = max(1, ctx_count // NV)
    item_count = NV * column_parts
    part_width = DV // column_parts
    sent_maps = jnp.repeat(local_map, column_parts, axis=1)[None]
    sent_bias = jnp.moveaxis(local_bias.reshape(groups, NV, DK, column_parts, part_width), 3, 2)
    sent_bias = sent_bias.reshape(groups, item_count, DK, part_width)[None]
    got_both = lax.all_to_all(
        jnp.concatenate([sent_maps, sent_bias], axis=-1),
        "ctx",
        split_axis=2,
        concat_axis=0,
        tiled=True,
    )
    got_maps = got_both[..., :DK]
    got_bias = got_both[..., DK:]

    def chain_step(state_now, incoming):
        return (chain_product(incoming[0], state_now) + incoming[1], state_now)

    _, entering_parts = lax.scan(
        chain_step, jnp.zeros(got_bias.shape[1:], jnp.float32), (got_maps, got_bias)
    )
    returned_states = lax.all_to_all(
        entering_parts, "ctx", split_axis=0, concat_axis=2, tiled=True
    )
    entering = returned_states[0].reshape(groups, NV, column_parts, DK, part_width)
    entering = jnp.moveaxis(entering, 2, 3).reshape(groups, NV, DK, DV)
    _, outputs = lax.scan(block_apply, entering, parts)
    outputs = jnp.transpose(outputs, (1, 0, 3, 2, 4)).reshape(groups, positions, NV, DV)
    normed_out = rms_rows(outputs, gain_out).reshape(groups, positions, NV * DV)
    outcome = (section_input.astype(jnp.float32) + normed_out).astype(jnp.bfloat16)
    return outcome


def solution(mesh):
    return jax.shard_map(
        local,
        mesh=mesh,
        in_specs=(
            P("dp", "ctx", None),
            P("section", "ctx", None),
            P("section", "ctx", None),
            P("section", None),
            P("section", None, None),
            P("section", None),
            P("section", None),
            P("section", None),
        ),
        out_specs=P(("dp", "section"), "ctx", None),
        check_vma=False,
    )
```

```python
import jax
import jax.numpy as jnp
from jax import lax
from jax.sharding import PartitionSpec as P

NK = 8
NV = 16
DK = 128
DV = 128
CONV = 4
BLOCK = 128


PRECISE = lax.Precision.HIGHEST


def from_behind(value, axis, by):
    length = lax.axis_size(axis)
    pairs = [(i, i + by) for i in range(length) if 0 <= i + by < length]
    return lax.ppermute(value, axis, pairs)


def rms_rows(values, gain_row):
    inverse = lax.rsqrt(jnp.mean(values * values, axis=-1, keepdims=True) + 1e-06)
    return values * inverse * gain_row


def unit_rows(values):
    return values * lax.rsqrt(jnp.sum(values * values, axis=-1, keepdims=True) + 1e-06)


def conv_rows(padded, conv_taps):
    tap_count = conv_taps.shape[0]
    length = padded.shape[-2] - tap_count + 1
    running_sum = jnp.zeros(padded.shape[:-2] + (length, padded.shape[-1]), jnp.float32)
    for offset in range(tap_count):
        running_sum = running_sum + conv_taps[offset].astype(jnp.float32) * padded[
            ..., offset : offset + length, :
        ].astype(jnp.float32)
    return jax.nn.silu(running_sum).astype(jnp.bfloat16)


def head_inputs(mixed_qk, mixed_v, gate_raw, decay_rates, biases):
    row_count = mixed_qk.shape[0]
    features = mixed_qk.astype(jnp.float32)
    queries = unit_rows(features[:, : NK * DK].reshape(row_count, NK, DK)) * DK ** (-0.5)
    key_rows = unit_rows(features[:, NK * DK : 2 * NK * DK].reshape(row_count, NK, DK))
    values = mixed_v.astype(jnp.float32).reshape(row_count, NV, DV)
    queries = jnp.repeat(queries, NV // NK, axis=1)
    key_rows = jnp.repeat(key_rows, NV // NK, axis=1)
    gate_float = gate_raw.astype(jnp.float32)
    strength = jax.nn.sigmoid(gate_float[:, :NV])
    logdecay = -decay_rates * jax.nn.softplus(gate_float[:, NV:] + biases)
    return (queries, key_rows, values, strength, logdecay)


def unit_lower_inverse(strict_part):
    size = strict_part.shape[-1]
    base = min(8, size)
    count = size // base
    lead = strict_part.shape[:-2]
    tiles = strict_part.reshape(lead + (count, base, count, base))
    diag_tiles = jnp.moveaxis(jnp.diagonal(tiles, axis1=-4, axis2=-2), -1, -3)
    identity = jnp.eye(base, dtype=strict_part.dtype)
    inverse = identity - diag_tiles
    power = diag_tiles
    reach = 2
    while reach < base:
        power = jnp.einsum("...ij,...jk->...ik", power, power, precision=PRECISE)
        inverse = inverse + jnp.einsum("...ij,...jk->...ik", inverse, power, precision=PRECISE)
        reach *= 2
    width = base
    while width < size:
        pairs = size // (2 * width)
        tiles = strict_part.reshape(lead + (pairs, 2 * width, pairs, 2 * width))
        below = jnp.moveaxis(jnp.diagonal(tiles, axis1=-4, axis2=-2), -1, -3)[
            ..., width:, :width
        ]
        inverse = inverse.reshape(lead + (pairs, 2, width, width))
        upper = inverse[..., 0, :, :]
        lower = inverse[..., 1, :, :]
        corner = -jnp.einsum(
            "...ij,...jk->...ik",
            lower,
            jnp.einsum("...ij,...jk->...ik", below, upper, precision=PRECISE),
            precision=PRECISE,
        )
        zeros = jnp.zeros_like(upper)
        top = jnp.concatenate([upper, zeros], axis=-1)
        bottom = jnp.concatenate([corner, lower], axis=-1)
        inverse = jnp.concatenate([top, bottom], axis=-2)
        width *= 2
    return inverse.reshape(lead + (size, size))


def block_parts(queries, key_rows, values, strength, logdecay):
    block_len = queries.shape[1]
    cumulative = jnp.swapaxes(jnp.cumsum(logdecay, axis=1), 1, 2)
    beta_heads = jnp.swapaxes(strength, 1, 2)
    query_heads = jnp.swapaxes(queries, 1, 2)
    key_heads = jnp.swapaxes(key_rows, 1, 2)
    value_heads = jnp.swapaxes(values, 1, 2)
    places = jnp.arange(block_len)
    lower_mask = places[:, None] >= places[None, :]
    strict_mask = places[:, None] > places[None, :]
    log_gap = cumulative[..., :, None] - cumulative[..., None, :]
    decay_ratio = jnp.where(lower_mask, jnp.exp(jnp.where(lower_mask, log_gap, 0.0)), 0.0)
    key_inner = jnp.einsum("nhid,nhjd->nhij", key_heads, key_heads, precision=PRECISE)
    strict_part = jnp.where(strict_mask, beta_heads[..., :, None] * key_inner * decay_ratio, 0.0)
    gamma_rows = jnp.exp(cumulative)
    inverse = unit_lower_inverse(strict_part)
    mixing = jnp.einsum(
        "...ij,...jk->...ik",
        inverse,
        (beta_heads * gamma_rows)[..., None] * key_heads,
        precision=PRECISE,
    )
    fresh_rows = jnp.einsum(
        "...ij,...jk->...ik", inverse, beta_heads[..., None] * value_heads, precision=PRECISE
    )
    scores = jnp.einsum("nhid,nhjd->nhij", query_heads, key_heads, precision=PRECISE) * decay_ratio
    qgamma = gamma_rows[..., None] * query_heads
    key_tail = jnp.exp(cumulative[..., -1:] - cumulative)[..., None] * key_heads
    block_decay = gamma_rows[..., -1]
    return (fresh_rows, mixing, scores, qgamma, key_tail, block_decay)


def block_apply(state_now, block_items):
    fresh_rows, mixing, scores, qgamma, key_tail, block_decay = block_items
    update = fresh_rows - jnp.einsum("...cd,...de->...ce", mixing, state_now, precision=PRECISE)
    output = jnp.einsum("...cd,...de->...ce", qgamma, state_now, precision=PRECISE) + jnp.einsum(
        "...ij,...je->...ie", scores, update, precision=PRECISE
    )
    state_next = block_decay[..., None, None] * state_now + jnp.einsum(
        "...cd,...ce->...de", key_tail, update, precision=PRECISE
    )
    return (state_next, output)


def chain_product(left_map, right_map):
    return jnp.einsum("...ij,...jk->...ik", left_map, right_map, precision=PRECISE)


def local(tokens, w_qkv, w_gate, norm_gain, conv_weight, decay_rate, dt_bias, head_gain):
    section = lax.axis_index("section")
    layer_count = lax.axis_size("section")

    def every_layer(value):
        held = [value]
        for offset in range(1, layer_count):
            pairs = [(i, (i + offset) % layer_count) for i in range(layer_count)]
            held.append(lax.ppermute(value, "section", pairs))
        layers = []
        for layer_index in range(layer_count):
            owner_offset = (section - layer_index) % layer_count
            chosen = held[0]
            for offset in range(1, layer_count):
                chosen = jnp.where(owner_offset == offset, held[offset], chosen)
            layers.append(chosen[0])
        return layers

    qk_width = 2 * NK * DK
    all_first = every_layer(jnp.concatenate([w_qkv[..., :qk_width], w_gate], axis=2))
    all_second = every_layer(w_qkv[..., qk_width:])
    all_gain_in = every_layer(norm_gain)
    all_taps = every_layer(conv_weight)
    all_rates = every_layer(decay_rate)
    all_biases = every_layer(dt_bias)
    all_gain_out = every_layer(head_gain)
    hidden = lax.dynamic_slice_in_dim(tokens, section, 1, axis=0)
    arrived = None
    for layer_index in range(layer_count):
        first_shard = all_first[layer_index]
        if arrived is not None:
            arrived, first_shard = lax.optimization_barrier((arrived, first_shard))
        full_first = lax.all_gather(first_shard, "ctx", axis=0, tiled=True)
        full_first, second_shard = lax.optimization_barrier((full_first, all_second[layer_index]))
        full_second = lax.all_gather(second_shard, "ctx", axis=0, tiled=True)
        hidden, arrived = layer_apply(
            hidden,
            full_first,
            full_second,
            all_gain_in[layer_index],
            all_taps[layer_index],
            all_rates[layer_index],
            all_biases[layer_index],
            all_gain_out[layer_index],
        )
    return hidden


def layer_apply(section_input, full_first, full_second, gain_in, conv_taps, decay_rates, biases, gain_out):
    groups, positions, model_width = section_input.shape
    blocks = positions // BLOCK
    layer_normed = (
        rms_rows(section_input.astype(jnp.float32), gain_in)
        .astype(jnp.bfloat16)
        .reshape(groups * positions, model_width)
    )
    projected = jnp.dot(layer_normed, full_first, preferred_element_type=jnp.float32)
    qk_width = full_first.shape[1] - 2 * NV
    features_qk = projected[:, :qk_width].astype(jnp.bfloat16).reshape(groups, positions, qk_width)
    gate_raw = projected[:, qk_width:].astype(jnp.bfloat16)
    proj_v = jnp.dot(layer_normed, full_second, preferred_element_type=jnp.float32)
    features_v = proj_v.astype(jnp.bfloat16).reshape(groups, positions, proj_v.shape[1])

    def mixed_part(features, taps):
        previous_rows = from_behind(features[:, positions - (CONV - 1) :], "ctx", 1)
        mixed = conv_rows(jnp.concatenate([previous_rows, features], axis=1), taps)
        return mixed.reshape(groups * positions, mixed.shape[2])

    queries, key_rows, values, strength, logdecay = head_inputs(
        mixed_part(features_qk, conv_taps[:, :qk_width]),
        mixed_part(features_v, conv_taps[:, qk_width:]),
        gate_raw,
        decay_rates,
        biases,
    )
    count_blocks = groups * blocks
    parts = block_parts(
        queries.reshape(count_blocks, BLOCK, NV, DK),
        key_rows.reshape(count_blocks, BLOCK, NV, DK),
        values.reshape(count_blocks, BLOCK, NV, DV),
        strength.reshape(count_blocks, BLOCK, NV),
        logdecay.reshape(count_blocks, BLOCK, NV),
    )
    parts = tuple(
        (
            jnp.moveaxis(source.reshape((groups, blocks) + source.shape[1:]), 1, 0)
            for source in parts
        )
    )
    fresh_rows, mixing, scores, qgamma, key_tail, block_decay = parts
    identity = jnp.broadcast_to(jnp.eye(DK, dtype=jnp.float32), (groups, NV, DK, DK))
    no_state = jnp.zeros((groups, NV, DK, DV), jnp.float32)
    step_maps = block_decay[..., None, None] * identity - jnp.einsum(
        "...cd,...cf->...df", key_tail, mixing, precision=PRECISE
    )
    step_biases = jnp.einsum("...cd,...ce->...de", key_tail, fresh_rows, precision=PRECISE)

    def compose(running, block_items):
        map_now, bias_now = running
        step_map, step_bias = block_items
        return (
            (chain_product(step_map, map_now), chain_product(step_map, bias_now) + step_bias),
            None,
        )

    (local_map, local_bias), _ = lax.scan(
        compose, (identity, no_state), (step_maps, step_biases)
    )
    ctx_count = lax.axis_size("ctx")
    column_parts = max(1, ctx_count // NV)
    item_count = NV * column_parts
    part_width = DV // column_parts
    sent_maps = jnp.repeat(local_map, column_parts, axis=1)[None]
    sent_bias = jnp.moveaxis(local_bias.reshape(groups, NV, DK, column_parts, part_width), 3, 2)
    sent_bias = sent_bias.reshape(groups, item_count, DK, part_width)[None]
    got_maps = lax.all_to_all(sent_maps, "ctx", split_axis=2, concat_axis=0, tiled=True)
    got_bias = lax.all_to_all(sent_bias, "ctx", split_axis=2, concat_axis=0, tiled=True)

    def chain_step(state_now, incoming):
        return (chain_product(incoming[0], state_now) + incoming[1], state_now)

    _, entering_parts = lax.scan(
        chain_step, jnp.zeros(got_bias.shape[1:], jnp.float32), (got_maps, got_bias)
    )
    returned_states = lax.all_to_all(
        entering_parts, "ctx", split_axis=0, concat_axis=2, tiled=True
    )
    entering = returned_states[0].reshape(groups, NV, column_parts, DK, part_width)
    entering = jnp.moveaxis(entering, 2, 3).reshape(groups, NV, DK, DV)
    _, outputs = lax.scan(block_apply, entering, parts)
    outputs = jnp.transpose(outputs, (1, 0, 3, 2, 4)).reshape(groups, positions, NV, DV)
    normed_out = rms_rows(outputs, gain_out).reshape(groups, positions, NV * DV)
    outcome = (section_input.astype(jnp.float32) + normed_out).astype(jnp.bfloat16)
    return outcome, step_biases


def solution(mesh):
    return jax.shard_map(
        local,
        mesh=mesh,
        in_specs=(
            P("dp", "ctx", None),
            P("section", "ctx", None),
            P("section", "ctx", None),
            P("section", None),
            P("section", None, None),
            P("section", None),
            P("section", None),
            P("section", None),
        ),
        out_specs=P(("dp", "section"), "ctx", None),
        check_vma=False,
    )
```

```python
import jax
import jax.numpy as jnp
from jax import lax
from jax.sharding import PartitionSpec as P

NK = 8
NV = 16
DK = 128
DV = 128
CONV = 4
BLOCK = 128


PRECISE = lax.Precision.HIGHEST


def from_behind(value, axis, by):
    length = lax.axis_size(axis)
    pairs = [(i, i + by) for i in range(length) if 0 <= i + by < length]
    return lax.ppermute(value, axis, pairs)


def rms_rows(values, gain_row):
    inverse = lax.rsqrt(jnp.mean(values * values, axis=-1, keepdims=True) + 1e-06)
    return values * inverse * gain_row


def unit_rows(values):
    return values * lax.rsqrt(jnp.sum(values * values, axis=-1, keepdims=True) + 1e-06)


def conv_rows(padded, conv_taps):
    tap_count = conv_taps.shape[0]
    length = padded.shape[-2] - tap_count + 1
    running_sum = jnp.zeros(padded.shape[:-2] + (length, padded.shape[-1]), jnp.float32)
    for offset in range(tap_count):
        running_sum = running_sum + conv_taps[offset].astype(jnp.float32) * padded[
            ..., offset : offset + length, :
        ].astype(jnp.float32)
    return jax.nn.silu(running_sum).astype(jnp.bfloat16)


def head_inputs(mixed_qk, mixed_v, gate_raw, decay_rates, biases):
    row_count = mixed_qk.shape[0]
    features = mixed_qk.astype(jnp.float32)
    queries = unit_rows(features[:, : NK * DK].reshape(row_count, NK, DK)) * DK ** (-0.5)
    key_rows = unit_rows(features[:, NK * DK : 2 * NK * DK].reshape(row_count, NK, DK))
    values = mixed_v.astype(jnp.float32).reshape(row_count, NV, DV)
    queries = jnp.repeat(queries, NV // NK, axis=1)
    key_rows = jnp.repeat(key_rows, NV // NK, axis=1)
    gate_float = gate_raw.astype(jnp.float32)
    strength = jax.nn.sigmoid(gate_float[:, :NV])
    logdecay = -decay_rates * jax.nn.softplus(gate_float[:, NV:] + biases)
    return (queries, key_rows, values, strength, logdecay)


def unit_lower_inverse(strict_part):
    size = strict_part.shape[-1]
    base = min(8, size)
    count = size // base
    lead = strict_part.shape[:-2]
    tiles = strict_part.reshape(lead + (count, base, count, base))
    diag_tiles = jnp.moveaxis(jnp.diagonal(tiles, axis1=-4, axis2=-2), -1, -3)
    identity = jnp.eye(base, dtype=strict_part.dtype)
    inverse = identity - diag_tiles
    power = diag_tiles
    reach = 2
    while reach < base:
        power = jnp.einsum("...ij,...jk->...ik", power, power, precision=PRECISE)
        inverse = inverse + jnp.einsum("...ij,...jk->...ik", inverse, power, precision=PRECISE)
        reach *= 2
    width = base
    while width < size:
        pairs = size // (2 * width)
        tiles = strict_part.reshape(lead + (pairs, 2 * width, pairs, 2 * width))
        below = jnp.moveaxis(jnp.diagonal(tiles, axis1=-4, axis2=-2), -1, -3)[
            ..., width:, :width
        ]
        inverse = inverse.reshape(lead + (pairs, 2, width, width))
        upper = inverse[..., 0, :, :]
        lower = inverse[..., 1, :, :]
        corner = -jnp.einsum(
            "...ij,...jk->...ik",
            lower,
            jnp.einsum("...ij,...jk->...ik", below, upper, precision=PRECISE),
            precision=PRECISE,
        )
        zeros = jnp.zeros_like(upper)
        top = jnp.concatenate([upper, zeros], axis=-1)
        bottom = jnp.concatenate([corner, lower], axis=-1)
        inverse = jnp.concatenate([top, bottom], axis=-2)
        width *= 2
    return inverse.reshape(lead + (size, size))


def block_parts(queries, key_rows, values, strength, logdecay):
    block_len = queries.shape[1]
    cumulative = jnp.swapaxes(jnp.cumsum(logdecay, axis=1), 1, 2)
    beta_heads = jnp.swapaxes(strength, 1, 2)
    query_heads = jnp.swapaxes(queries, 1, 2)
    key_heads = jnp.swapaxes(key_rows, 1, 2)
    value_heads = jnp.swapaxes(values, 1, 2)
    places = jnp.arange(block_len)
    lower_mask = places[:, None] >= places[None, :]
    strict_mask = places[:, None] > places[None, :]
    log_gap = cumulative[..., :, None] - cumulative[..., None, :]
    decay_ratio = jnp.where(lower_mask, jnp.exp(jnp.where(lower_mask, log_gap, 0.0)), 0.0)
    key_inner = jnp.einsum("nhid,nhjd->nhij", key_heads, key_heads, precision=PRECISE)
    strict_part = jnp.where(strict_mask, beta_heads[..., :, None] * key_inner * decay_ratio, 0.0)
    gamma_rows = jnp.exp(cumulative)
    inverse = unit_lower_inverse(strict_part)
    mixing = jnp.einsum(
        "...ij,...jk->...ik",
        inverse,
        (beta_heads * gamma_rows)[..., None] * key_heads,
        precision=PRECISE,
    )
    fresh_rows = jnp.einsum(
        "...ij,...jk->...ik", inverse, beta_heads[..., None] * value_heads, precision=PRECISE
    )
    scores = jnp.einsum("nhid,nhjd->nhij", query_heads, key_heads, precision=PRECISE) * decay_ratio
    qgamma = gamma_rows[..., None] * query_heads
    key_tail = jnp.exp(cumulative[..., -1:] - cumulative)[..., None] * key_heads
    block_decay = gamma_rows[..., -1]
    return (fresh_rows, mixing, scores, qgamma, key_tail, block_decay)


def block_apply(state_now, block_items):
    fresh_rows, mixing, scores, qgamma, key_tail, block_decay = block_items
    update = fresh_rows - jnp.einsum("...cd,...de->...ce", mixing, state_now, precision=PRECISE)
    output = jnp.einsum("...cd,...de->...ce", qgamma, state_now, precision=PRECISE) + jnp.einsum(
        "...ij,...je->...ie", scores, update, precision=PRECISE
    )
    state_next = block_decay[..., None, None] * state_now + jnp.einsum(
        "...cd,...ce->...de", key_tail, update, precision=PRECISE
    )
    return (state_next, output)


def chain_product(left_map, right_map):
    return jnp.einsum("...ij,...jk->...ik", left_map, right_map, precision=PRECISE)


def local(tokens, w_qkv, w_gate, norm_gain, conv_weight, decay_rate, dt_bias, head_gain):
    section = lax.axis_index("section")
    layer_count = lax.axis_size("section")

    def every_layer(value):
        held = [value]
        for offset in range(1, layer_count):
            pairs = [(i, (i + offset) % layer_count) for i in range(layer_count)]
            held.append(lax.ppermute(value, "section", pairs))
        layers = []
        for layer_index in range(layer_count):
            owner_offset = (section - layer_index) % layer_count
            chosen = held[0]
            for offset in range(1, layer_count):
                chosen = jnp.where(owner_offset == offset, held[offset], chosen)
            layers.append(chosen[0])
        return layers

    qk_width = 2 * NK * DK
    all_first = every_layer(jnp.concatenate([w_qkv[..., :qk_width], w_gate], axis=2))
    all_second = every_layer(w_qkv[..., qk_width:])
    all_gain_in = every_layer(norm_gain)
    all_taps = every_layer(conv_weight)
    all_rates = every_layer(decay_rate)
    all_biases = every_layer(dt_bias)
    all_gain_out = every_layer(head_gain)
    hidden = lax.dynamic_slice_in_dim(tokens, section, 1, axis=0)
    arrived = None
    for layer_index in range(layer_count):
        first_shard = all_first[layer_index]
        if arrived is not None:
            arrived, first_shard = lax.optimization_barrier((arrived, first_shard))
        full_first = lax.all_gather(first_shard, "ctx", axis=0, tiled=True)
        full_first, second_shard = lax.optimization_barrier((full_first, all_second[layer_index]))
        full_second = lax.all_gather(second_shard, "ctx", axis=0, tiled=True)
        hidden, arrived = layer_apply(
            hidden,
            full_first,
            full_second,
            all_gain_in[layer_index],
            all_taps[layer_index],
            all_rates[layer_index],
            all_biases[layer_index],
            all_gain_out[layer_index],
        )
    return hidden


def layer_apply(section_input, full_first, full_second, gain_in, conv_taps, decay_rates, biases, gain_out):
    groups, positions, model_width = section_input.shape
    blocks = positions // BLOCK
    own_normed = rms_rows(section_input.astype(jnp.float32), gain_in).astype(jnp.bfloat16)
    previous_normed = from_behind(own_normed[:, positions - (CONV - 1) :], "ctx", 1)
    extended = jnp.concatenate([previous_normed, own_normed], axis=1)
    extended_rows = extended.shape[1]
    layer_normed = extended.reshape(groups * extended_rows, model_width)
    projected = jnp.dot(layer_normed, full_first, preferred_element_type=jnp.float32)
    qk_width = full_first.shape[1] - 2 * NV
    projected = projected.reshape(groups, extended_rows, projected.shape[1])
    features_qk = projected[:, :, :qk_width].astype(jnp.bfloat16)
    gate_raw = projected[:, CONV - 1 :, qk_width:].astype(jnp.bfloat16).reshape(groups * positions, 2 * NV)
    proj_v = jnp.dot(layer_normed, full_second, preferred_element_type=jnp.float32)
    features_v = proj_v.astype(jnp.bfloat16).reshape(groups, extended_rows, proj_v.shape[1])

    def mixed_part(features, taps):
        mixed = conv_rows(features, taps)
        return mixed.reshape(groups * positions, mixed.shape[2])

    queries, key_rows, values, strength, logdecay = head_inputs(
        mixed_part(features_qk, conv_taps[:, :qk_width]),
        mixed_part(features_v, conv_taps[:, qk_width:]),
        gate_raw,
        decay_rates,
        biases,
    )
    count_blocks = groups * blocks
    parts = block_parts(
        queries.reshape(count_blocks, BLOCK, NV, DK),
        key_rows.reshape(count_blocks, BLOCK, NV, DK),
        values.reshape(count_blocks, BLOCK, NV, DV),
        strength.reshape(count_blocks, BLOCK, NV),
        logdecay.reshape(count_blocks, BLOCK, NV),
    )
    parts = tuple(
        (
            jnp.moveaxis(source.reshape((groups, blocks) + source.shape[1:]), 1, 0)
            for source in parts
        )
    )
    fresh_rows, mixing, scores, qgamma, key_tail, block_decay = parts
    identity = jnp.broadcast_to(jnp.eye(DK, dtype=jnp.float32), (groups, NV, DK, DK))
    no_state = jnp.zeros((groups, NV, DK, DV), jnp.float32)
    step_maps = block_decay[..., None, None] * identity - jnp.einsum(
        "...cd,...cf->...df", key_tail, mixing, precision=PRECISE
    )
    step_biases = jnp.einsum("...cd,...ce->...de", key_tail, fresh_rows, precision=PRECISE)

    def compose(running, block_items):
        map_now, bias_now = running
        step_map, step_bias = block_items
        return (
            (chain_product(step_map, map_now), chain_product(step_map, bias_now) + step_bias),
            None,
        )

    (local_map, local_bias), _ = lax.scan(
        compose, (identity, no_state), (step_maps, step_biases)
    )
    ctx_count = lax.axis_size("ctx")
    column_parts = max(1, ctx_count // NV)
    item_count = NV * column_parts
    part_width = DV // column_parts
    sent_maps = jnp.repeat(local_map, column_parts, axis=1)[None]
    sent_bias = jnp.moveaxis(local_bias.reshape(groups, NV, DK, column_parts, part_width), 3, 2)
    sent_bias = sent_bias.reshape(groups, item_count, DK, part_width)[None]
    got_maps = lax.all_to_all(sent_maps, "ctx", split_axis=2, concat_axis=0, tiled=True)
    got_bias = lax.all_to_all(sent_bias, "ctx", split_axis=2, concat_axis=0, tiled=True)

    def chain_step(state_now, incoming):
        return (chain_product(incoming[0], state_now) + incoming[1], state_now)

    _, entering_parts = lax.scan(
        chain_step, jnp.zeros(got_bias.shape[1:], jnp.float32), (got_maps, got_bias)
    )
    returned_states = lax.all_to_all(
        entering_parts, "ctx", split_axis=0, concat_axis=2, tiled=True
    )
    entering = returned_states[0].reshape(groups, NV, column_parts, DK, part_width)
    entering = jnp.moveaxis(entering, 2, 3).reshape(groups, NV, DK, DV)
    _, outputs = lax.scan(block_apply, entering, parts)
    outputs = jnp.transpose(outputs, (1, 0, 3, 2, 4)).reshape(groups, positions, NV, DV)
    normed_out = rms_rows(outputs, gain_out).reshape(groups, positions, NV * DV)
    outcome = (section_input.astype(jnp.float32) + normed_out).astype(jnp.bfloat16)
    return outcome, step_biases


def solution(mesh):
    return jax.shard_map(
        local,
        mesh=mesh,
        in_specs=(
            P("dp", "ctx", None),
            P("section", "ctx", None),
            P("section", "ctx", None),
            P("section", None),
            P("section", None, None),
            P("section", None),
            P("section", None),
            P("section", None),
        ),
        out_specs=P(("dp", "section"), "ctx", None),
        check_vma=False,
    )
```

```python
import jax
import jax.numpy as jnp
from jax import lax
from jax.sharding import PartitionSpec as P

NK = 8
NV = 16
DK = 128
DV = 128
CONV = 4
BLOCK = 128


PRECISE = lax.Precision.HIGHEST


def from_behind(value, axis, by):
    length = lax.axis_size(axis)
    pairs = [(i, i + by) for i in range(length) if 0 <= i + by < length]
    return lax.ppermute(value, axis, pairs)


def rms_rows(values, gain_row):
    inverse = lax.rsqrt(jnp.mean(values * values, axis=-1, keepdims=True) + 1e-06)
    return values * inverse * gain_row


def unit_rows(values):
    return values * lax.rsqrt(jnp.sum(values * values, axis=-1, keepdims=True) + 1e-06)


def conv_rows(padded, conv_taps):
    tap_count = conv_taps.shape[0]
    length = padded.shape[-2] - tap_count + 1
    running_sum = jnp.zeros(padded.shape[:-2] + (length, padded.shape[-1]), jnp.float32)
    for offset in range(tap_count):
        running_sum = running_sum + conv_taps[offset].astype(jnp.float32) * padded[
            ..., offset : offset + length, :
        ].astype(jnp.float32)
    return jax.nn.silu(running_sum).astype(jnp.bfloat16)


def head_inputs(mixed_qk, mixed_v, gate_raw, decay_rates, biases):
    row_count = mixed_qk.shape[0]
    features = mixed_qk.astype(jnp.float32)
    queries = unit_rows(features[:, : NK * DK].reshape(row_count, NK, DK)) * DK ** (-0.5)
    key_rows = unit_rows(features[:, NK * DK : 2 * NK * DK].reshape(row_count, NK, DK))
    values = mixed_v.astype(jnp.float32).reshape(row_count, NV, DV)
    queries = jnp.repeat(queries, NV // NK, axis=1)
    key_rows = jnp.repeat(key_rows, NV // NK, axis=1)
    gate_float = gate_raw.astype(jnp.float32)
    strength = jax.nn.sigmoid(gate_float[:, :NV])
    logdecay = -decay_rates * jax.nn.softplus(gate_float[:, NV:] + biases)
    return (queries, key_rows, values, strength, logdecay)


def unit_lower_inverse(strict_part):
    size = strict_part.shape[-1]
    base = min(8, size)
    count = size // base
    lead = strict_part.shape[:-2]
    tiles = strict_part.reshape(lead + (count, base, count, base))
    diag_tiles = jnp.moveaxis(jnp.diagonal(tiles, axis1=-4, axis2=-2), -1, -3)
    identity = jnp.eye(base, dtype=strict_part.dtype)
    inverse = identity - diag_tiles
    power = diag_tiles
    reach = 2
    while reach < base:
        power = jnp.einsum("...ij,...jk->...ik", power, power, precision=PRECISE)
        inverse = inverse + jnp.einsum("...ij,...jk->...ik", inverse, power, precision=PRECISE)
        reach *= 2
    width = base
    while width < size:
        pairs = size // (2 * width)
        tiles = strict_part.reshape(lead + (pairs, 2 * width, pairs, 2 * width))
        below = jnp.moveaxis(jnp.diagonal(tiles, axis1=-4, axis2=-2), -1, -3)[
            ..., width:, :width
        ]
        inverse = inverse.reshape(lead + (pairs, 2, width, width))
        upper = inverse[..., 0, :, :]
        lower = inverse[..., 1, :, :]
        corner = -jnp.einsum(
            "...ij,...jk->...ik",
            lower,
            jnp.einsum("...ij,...jk->...ik", below, upper, precision=PRECISE),
            precision=PRECISE,
        )
        zeros = jnp.zeros_like(upper)
        top = jnp.concatenate([upper, zeros], axis=-1)
        bottom = jnp.concatenate([corner, lower], axis=-1)
        inverse = jnp.concatenate([top, bottom], axis=-2)
        width *= 2
    return inverse.reshape(lead + (size, size))


def block_parts(queries, key_rows, values, strength, logdecay):
    block_len = queries.shape[1]
    cumulative = jnp.swapaxes(jnp.cumsum(logdecay, axis=1), 1, 2)
    beta_heads = jnp.swapaxes(strength, 1, 2)
    query_heads = jnp.swapaxes(queries, 1, 2)
    key_heads = jnp.swapaxes(key_rows, 1, 2)
    value_heads = jnp.swapaxes(values, 1, 2)
    places = jnp.arange(block_len)
    lower_mask = places[:, None] >= places[None, :]
    strict_mask = places[:, None] > places[None, :]
    log_gap = cumulative[..., :, None] - cumulative[..., None, :]
    decay_ratio = jnp.where(lower_mask, jnp.exp(jnp.where(lower_mask, log_gap, 0.0)), 0.0)
    key_inner = jnp.einsum("nhid,nhjd->nhij", key_heads, key_heads, precision=PRECISE)
    strict_part = jnp.where(strict_mask, beta_heads[..., :, None] * key_inner * decay_ratio, 0.0)
    gamma_rows = jnp.exp(cumulative)
    inverse = unit_lower_inverse(strict_part)
    mixing = jnp.einsum(
        "...ij,...jk->...ik",
        inverse,
        (beta_heads * gamma_rows)[..., None] * key_heads,
        precision=PRECISE,
    )
    fresh_rows = jnp.einsum(
        "...ij,...jk->...ik", inverse, beta_heads[..., None] * value_heads, precision=PRECISE
    )
    scores = jnp.einsum("nhid,nhjd->nhij", query_heads, key_heads, precision=PRECISE) * decay_ratio
    qgamma = gamma_rows[..., None] * query_heads
    key_tail = jnp.exp(cumulative[..., -1:] - cumulative)[..., None] * key_heads
    block_decay = gamma_rows[..., -1]
    return (fresh_rows, mixing, scores, qgamma, key_tail, block_decay)


def block_apply(state_now, block_items):
    fresh_rows, mixing, scores, qgamma, key_tail, block_decay = block_items
    update = fresh_rows - jnp.einsum("...cd,...de->...ce", mixing, state_now, precision=PRECISE)
    output = jnp.einsum("...cd,...de->...ce", qgamma, state_now, precision=PRECISE) + jnp.einsum(
        "...ij,...je->...ie", scores, update, precision=PRECISE
    )
    state_next = block_decay[..., None, None] * state_now + jnp.einsum(
        "...cd,...ce->...de", key_tail, update, precision=PRECISE
    )
    return (state_next, output)


def chain_product(left_map, right_map):
    return jnp.einsum("...ij,...jk->...ik", left_map, right_map, precision=PRECISE)


def local(tokens, w_qkv, w_gate, norm_gain, conv_weight, decay_rate, dt_bias, head_gain):
    section = lax.axis_index("section")
    layer_count = lax.axis_size("section")

    def every_layer(value):
        held = [value]
        for offset in range(1, layer_count):
            pairs = [(i, (i + offset) % layer_count) for i in range(layer_count)]
            held.append(lax.ppermute(value, "section", pairs))
        layers = []
        for layer_index in range(layer_count):
            owner_offset = (section - layer_index) % layer_count
            chosen = held[0]
            for offset in range(1, layer_count):
                chosen = jnp.where(owner_offset == offset, held[offset], chosen)
            layers.append(chosen[0])
        return layers

    qk_width = 2 * NK * DK
    all_first = every_layer(jnp.concatenate([w_qkv[..., :qk_width], w_gate], axis=2))
    all_second = every_layer(w_qkv[..., qk_width:])
    all_gain_in = every_layer(norm_gain)
    all_taps = every_layer(conv_weight)
    all_rates = every_layer(decay_rate)
    all_biases = every_layer(dt_bias)
    all_gain_out = every_layer(head_gain)
    hidden = lax.dynamic_slice_in_dim(tokens, section, 1, axis=0)
    gathered_next = None
    for layer_index in range(layer_count):
        full_first = lax.all_gather(all_first[layer_index], "ctx", axis=0, tiled=True)
        if gathered_next is None:
            full_first, second_shard = lax.optimization_barrier(
                (full_first, all_second[layer_index])
            )
            full_second = lax.all_gather(second_shard, "ctx", axis=0, tiled=True)
        else:
            full_second = gathered_next
        tie = all_second[layer_index + 1] if layer_index + 1 < layer_count else None
        hidden, tied = layer_apply(
            hidden,
            full_first,
            full_second,
            all_gain_in[layer_index],
            all_taps[layer_index],
            all_rates[layer_index],
            all_biases[layer_index],
            all_gain_out[layer_index],
            tie,
        )
        if tied is not None:
            gathered_next = lax.all_gather(tied, "ctx", axis=0, tiled=True)
    return hidden


def layer_apply(
    section_input, full_first, full_second, gain_in, conv_taps, decay_rates, biases, gain_out, tie
):
    groups, positions, model_width = section_input.shape
    blocks = positions // BLOCK
    own_normed = rms_rows(section_input.astype(jnp.float32), gain_in).astype(jnp.bfloat16)
    previous_normed = from_behind(own_normed[:, positions - (CONV - 1) :], "ctx", 1)
    extended = jnp.concatenate([previous_normed, own_normed], axis=1)
    extended_rows = extended.shape[1]
    layer_normed = extended.reshape(groups * extended_rows, model_width)
    projected = jnp.dot(layer_normed, full_first, preferred_element_type=jnp.float32)
    qk_width = full_first.shape[1] - 2 * NV
    projected = projected.reshape(groups, extended_rows, projected.shape[1])
    features_qk = projected[:, :, :qk_width].astype(jnp.bfloat16)
    gate_raw = projected[:, CONV - 1 :, qk_width:].astype(jnp.bfloat16).reshape(groups * positions, 2 * NV)
    proj_v = jnp.dot(layer_normed, full_second, preferred_element_type=jnp.float32)
    features_v = proj_v.astype(jnp.bfloat16).reshape(groups, extended_rows, proj_v.shape[1])

    def mixed_part(features, taps):
        mixed = conv_rows(features, taps)
        return mixed.reshape(groups * positions, mixed.shape[2])

    queries, key_rows, values, strength, logdecay = head_inputs(
        mixed_part(features_qk, conv_taps[:, :qk_width]),
        mixed_part(features_v, conv_taps[:, qk_width:]),
        gate_raw,
        decay_rates,
        biases,
    )
    count_blocks = groups * blocks
    parts = block_parts(
        queries.reshape(count_blocks, BLOCK, NV, DK),
        key_rows.reshape(count_blocks, BLOCK, NV, DK),
        values.reshape(count_blocks, BLOCK, NV, DV),
        strength.reshape(count_blocks, BLOCK, NV),
        logdecay.reshape(count_blocks, BLOCK, NV),
    )
    parts = tuple(
        (
            jnp.moveaxis(source.reshape((groups, blocks) + source.shape[1:]), 1, 0)
            for source in parts
        )
    )
    fresh_rows, mixing, scores, qgamma, key_tail, block_decay = parts
    identity = jnp.broadcast_to(jnp.eye(DK, dtype=jnp.float32), (groups, NV, DK, DK))
    no_state = jnp.zeros((groups, NV, DK, DV), jnp.float32)
    step_maps = block_decay[..., None, None] * identity - jnp.einsum(
        "...cd,...cf->...df", key_tail, mixing, precision=PRECISE
    )
    step_biases = jnp.einsum("...cd,...ce->...de", key_tail, fresh_rows, precision=PRECISE)

    def compose(running, block_items):
        map_now, bias_now = running
        step_map, step_bias = block_items
        return (
            (chain_product(step_map, map_now), chain_product(step_map, bias_now) + step_bias),
            None,
        )

    (local_map, local_bias), _ = lax.scan(
        compose, (identity, no_state), (step_maps, step_biases)
    )
    ctx_count = lax.axis_size("ctx")
    column_parts = max(1, ctx_count // NV)
    item_count = NV * column_parts
    part_width = DV // column_parts
    sent_maps = jnp.repeat(local_map, column_parts, axis=1)[None]
    sent_bias = jnp.moveaxis(local_bias.reshape(groups, NV, DK, column_parts, part_width), 3, 2)
    sent_bias = sent_bias.reshape(groups, item_count, DK, part_width)[None]
    got_maps = lax.all_to_all(sent_maps, "ctx", split_axis=2, concat_axis=0, tiled=True)
    got_bias = lax.all_to_all(sent_bias, "ctx", split_axis=2, concat_axis=0, tiled=True)

    def chain_step(state_now, incoming):
        return (chain_product(incoming[0], state_now) + incoming[1], state_now)

    _, entering_parts = lax.scan(
        chain_step, jnp.zeros(got_bias.shape[1:], jnp.float32), (got_maps, got_bias)
    )
    returned_states = lax.all_to_all(
        entering_parts, "ctx", split_axis=0, concat_axis=2, tiled=True
    )
    entering = returned_states[0].reshape(groups, NV, column_parts, DK, part_width)
    entering = jnp.moveaxis(entering, 2, 3).reshape(groups, NV, DK, DV)
    if tie is not None:
        entering, tie = lax.optimization_barrier((entering, tie))
    _, outputs = lax.scan(block_apply, entering, parts)
    outputs = jnp.transpose(outputs, (1, 0, 3, 2, 4)).reshape(groups, positions, NV, DV)
    normed_out = rms_rows(outputs, gain_out).reshape(groups, positions, NV * DV)
    outcome = (section_input.astype(jnp.float32) + normed_out).astype(jnp.bfloat16)
    return outcome, tie


def solution(mesh):
    return jax.shard_map(
        local,
        mesh=mesh,
        in_specs=(
            P("dp", "ctx", None),
            P("section", "ctx", None),
            P("section", "ctx", None),
            P("section", None),
            P("section", None, None),
            P("section", None),
            P("section", None),
            P("section", None),
        ),
        out_specs=P(("dp", "section"), "ctx", None),
        check_vma=False,
    )
```

```python
import jax
import jax.numpy as jnp
from jax import lax
from jax.sharding import PartitionSpec as P

NK = 8
NV = 16
DK = 128
DV = 128
CONV = 4
BLOCK = 128


PRECISE = lax.Precision.HIGHEST


def from_behind(value, axis, by):
    length = lax.axis_size(axis)
    pairs = [(i, i + by) for i in range(length) if 0 <= i + by < length]
    return lax.ppermute(value, axis, pairs)


def rms_rows(values, gain_row):
    inverse = lax.rsqrt(jnp.mean(values * values, axis=-1, keepdims=True) + 1e-06)
    return values * inverse * gain_row


def unit_rows(values):
    return values * lax.rsqrt(jnp.sum(values * values, axis=-1, keepdims=True) + 1e-06)


def conv_rows(padded, conv_taps):
    tap_count = conv_taps.shape[0]
    length = padded.shape[-2] - tap_count + 1
    running_sum = jnp.zeros(padded.shape[:-2] + (length, padded.shape[-1]), jnp.float32)
    for offset in range(tap_count):
        running_sum = running_sum + conv_taps[offset].astype(jnp.float32) * padded[
            ..., offset : offset + length, :
        ].astype(jnp.float32)
    return jax.nn.silu(running_sum).astype(jnp.bfloat16)


def head_inputs(mixed_qk, mixed_v, gate_raw, decay_rates, biases):
    row_count = mixed_qk.shape[0]
    features = mixed_qk.astype(jnp.float32)
    queries = unit_rows(features[:, : NK * DK].reshape(row_count, NK, DK)) * DK ** (-0.5)
    key_rows = unit_rows(features[:, NK * DK : 2 * NK * DK].reshape(row_count, NK, DK))
    values = mixed_v.astype(jnp.float32).reshape(row_count, NV, DV)
    queries = jnp.repeat(queries, NV // NK, axis=1)
    key_rows = jnp.repeat(key_rows, NV // NK, axis=1)
    gate_float = gate_raw.astype(jnp.float32)
    strength = jax.nn.sigmoid(gate_float[:, :NV])
    logdecay = -decay_rates * jax.nn.softplus(gate_float[:, NV:] + biases)
    return (queries, key_rows, values, strength, logdecay)


def unit_lower_inverse(strict_part):
    size = strict_part.shape[-1]
    base = min(8, size)
    count = size // base
    lead = strict_part.shape[:-2]
    tiles = strict_part.reshape(lead + (count, base, count, base))
    diag_tiles = jnp.moveaxis(jnp.diagonal(tiles, axis1=-4, axis2=-2), -1, -3)
    identity = jnp.eye(base, dtype=strict_part.dtype)
    inverse = identity - diag_tiles
    power = diag_tiles
    reach = 2
    while reach < base:
        power = jnp.einsum("...ij,...jk->...ik", power, power, precision=PRECISE)
        inverse = inverse + jnp.einsum("...ij,...jk->...ik", inverse, power, precision=PRECISE)
        reach *= 2
    width = base
    while width < size:
        pairs = size // (2 * width)
        tiles = strict_part.reshape(lead + (pairs, 2 * width, pairs, 2 * width))
        below = jnp.moveaxis(jnp.diagonal(tiles, axis1=-4, axis2=-2), -1, -3)[
            ..., width:, :width
        ]
        inverse = inverse.reshape(lead + (pairs, 2, width, width))
        upper = inverse[..., 0, :, :]
        lower = inverse[..., 1, :, :]
        corner = -jnp.einsum(
            "...ij,...jk->...ik",
            lower,
            jnp.einsum("...ij,...jk->...ik", below, upper, precision=PRECISE),
            precision=PRECISE,
        )
        zeros = jnp.zeros_like(upper)
        top = jnp.concatenate([upper, zeros], axis=-1)
        bottom = jnp.concatenate([corner, lower], axis=-1)
        inverse = jnp.concatenate([top, bottom], axis=-2)
        width *= 2
    return inverse.reshape(lead + (size, size))


def block_parts(queries, key_rows, values, strength, logdecay):
    block_len = queries.shape[1]
    cumulative = jnp.swapaxes(jnp.cumsum(logdecay, axis=1), 1, 2)
    beta_heads = jnp.swapaxes(strength, 1, 2)
    query_heads = jnp.swapaxes(queries, 1, 2)
    key_heads = jnp.swapaxes(key_rows, 1, 2)
    value_heads = jnp.swapaxes(values, 1, 2)
    places = jnp.arange(block_len)
    lower_mask = places[:, None] >= places[None, :]
    strict_mask = places[:, None] > places[None, :]
    log_gap = cumulative[..., :, None] - cumulative[..., None, :]
    decay_ratio = jnp.where(lower_mask, jnp.exp(jnp.where(lower_mask, log_gap, 0.0)), 0.0)
    key_inner = jnp.einsum("nhid,nhjd->nhij", key_heads, key_heads, precision=PRECISE)
    strict_part = jnp.where(strict_mask, beta_heads[..., :, None] * key_inner * decay_ratio, 0.0)
    gamma_rows = jnp.exp(cumulative)
    inverse = unit_lower_inverse(strict_part)
    mixing = jnp.einsum(
        "...ij,...jk->...ik",
        inverse,
        (beta_heads * gamma_rows)[..., None] * key_heads,
        precision=PRECISE,
    )
    fresh_rows = jnp.einsum(
        "...ij,...jk->...ik", inverse, beta_heads[..., None] * value_heads, precision=PRECISE
    )
    scores = jnp.einsum("nhid,nhjd->nhij", query_heads, key_heads, precision=PRECISE) * decay_ratio
    qgamma = gamma_rows[..., None] * query_heads
    key_tail = jnp.exp(cumulative[..., -1:] - cumulative)[..., None] * key_heads
    block_decay = gamma_rows[..., -1]
    return (fresh_rows, mixing, scores, qgamma, key_tail, block_decay)


def block_apply(state_now, block_items):
    fresh_rows, mixing, scores, qgamma, key_tail, block_decay = block_items
    update = fresh_rows - jnp.einsum("...cd,...de->...ce", mixing, state_now, precision=PRECISE)
    output = jnp.einsum("...cd,...de->...ce", qgamma, state_now, precision=PRECISE) + jnp.einsum(
        "...ij,...je->...ie", scores, update, precision=PRECISE
    )
    state_next = block_decay[..., None, None] * state_now + jnp.einsum(
        "...cd,...ce->...de", key_tail, update, precision=PRECISE
    )
    return (state_next, output)


def chain_product(left_map, right_map):
    return jnp.einsum("...ij,...jk->...ik", left_map, right_map, precision=PRECISE)


def local(tokens, w_qkv, w_gate, norm_gain, conv_weight, decay_rate, dt_bias, head_gain):
    section = lax.axis_index("section")
    layer_count = lax.axis_size("section")

    def every_layer(value):
        held = [value]
        for offset in range(1, layer_count):
            pairs = [(i, (i + offset) % layer_count) for i in range(layer_count)]
            held.append(lax.ppermute(value, "section", pairs))
        layers = []
        for layer_index in range(layer_count):
            owner_offset = (section - layer_index) % layer_count
            chosen = held[0]
            for offset in range(1, layer_count):
                chosen = jnp.where(owner_offset == offset, held[offset], chosen)
            layers.append(chosen[0])
        return layers

    qk_width = 2 * NK * DK
    all_first = every_layer(jnp.concatenate([w_qkv[..., :qk_width], w_gate], axis=2))
    all_second = every_layer(w_qkv[..., qk_width:])
    all_gain_in = every_layer(norm_gain)
    all_taps = every_layer(conv_weight)
    all_rates = every_layer(decay_rate)
    all_biases = every_layer(dt_bias)
    all_gain_out = every_layer(head_gain)
    hidden = lax.dynamic_slice_in_dim(tokens, section, 1, axis=0)
    gathered_next = None
    for layer_index in range(layer_count):
        full_first = lax.all_gather(all_first[layer_index], "ctx", axis=0, tiled=True)
        if gathered_next is None:
            full_first, second_shard = lax.optimization_barrier(
                (full_first, all_second[layer_index])
            )
            full_second = lax.all_gather(second_shard, "ctx", axis=0, tiled=True)
        else:
            full_second = gathered_next
        tie = all_second[layer_index + 1] if layer_index + 1 < layer_count else None
        hidden, tied = layer_apply(
            hidden,
            full_first,
            full_second,
            all_gain_in[layer_index],
            all_taps[layer_index],
            all_rates[layer_index],
            all_biases[layer_index],
            all_gain_out[layer_index],
            tie,
        )
        if tied is not None:
            gathered_next = lax.all_gather(tied, "ctx", axis=0, tiled=True)
    return hidden


def layer_apply(
    section_input, full_first, full_second, gain_in, conv_taps, decay_rates, biases, gain_out, tie
):
    groups, positions, model_width = section_input.shape
    blocks = positions // BLOCK
    own_normed = rms_rows(section_input.astype(jnp.float32), gain_in).astype(jnp.bfloat16)
    previous_normed = from_behind(own_normed[:, positions - (CONV - 1) :], "ctx", 1)
    extended = jnp.concatenate([previous_normed, own_normed], axis=1)
    extended_rows = extended.shape[1]
    layer_normed = extended.reshape(groups * extended_rows, model_width)
    projected = jnp.dot(layer_normed, full_first, preferred_element_type=jnp.float32)
    qk_width = full_first.shape[1] - 2 * NV
    projected = projected.reshape(groups, extended_rows, projected.shape[1])
    features_qk = projected[:, :, :qk_width].astype(jnp.bfloat16)
    gate_raw = projected[:, CONV - 1 :, qk_width:].astype(jnp.bfloat16).reshape(groups * positions, 2 * NV)
    proj_v = jnp.dot(layer_normed, full_second, preferred_element_type=jnp.float32)
    features_v = proj_v.astype(jnp.bfloat16).reshape(groups, extended_rows, proj_v.shape[1])

    def mixed_part(features, taps):
        mixed = conv_rows(features, taps)
        return mixed.reshape(groups * positions, mixed.shape[2])

    queries, key_rows, values, strength, logdecay = head_inputs(
        mixed_part(features_qk, conv_taps[:, :qk_width]),
        mixed_part(features_v, conv_taps[:, qk_width:]),
        gate_raw,
        decay_rates,
        biases,
    )
    count_blocks = groups * blocks
    parts = block_parts(
        queries.reshape(count_blocks, BLOCK, NV, DK),
        key_rows.reshape(count_blocks, BLOCK, NV, DK),
        values.reshape(count_blocks, BLOCK, NV, DV),
        strength.reshape(count_blocks, BLOCK, NV),
        logdecay.reshape(count_blocks, BLOCK, NV),
    )
    parts = tuple(
        (
            jnp.moveaxis(source.reshape((groups, blocks) + source.shape[1:]), 1, 0)
            for source in parts
        )
    )
    fresh_rows, mixing, scores, qgamma, key_tail, block_decay = parts
    identity = jnp.broadcast_to(jnp.eye(DK, dtype=jnp.float32), (groups, NV, DK, DK))
    no_state = jnp.zeros((groups, NV, DK, DV), jnp.float32)
    step_maps = block_decay[..., None, None] * identity - jnp.einsum(
        "...cd,...cf->...df", key_tail, mixing, precision=PRECISE
    )
    step_biases = jnp.einsum("...cd,...ce->...de", key_tail, fresh_rows, precision=PRECISE)

    def compose(running, block_items):
        map_now, bias_now = running
        step_map, step_bias = block_items
        return (
            (chain_product(step_map, map_now), chain_product(step_map, bias_now) + step_bias),
            None,
        )

    (local_map, local_bias), _ = lax.scan(
        compose, (identity, no_state), (step_maps, step_biases)
    )
    ctx_count = lax.axis_size("ctx")
    column_parts = max(1, ctx_count // NV)
    item_count = NV * column_parts
    part_width = DV // column_parts
    sent_maps = jnp.repeat(local_map, column_parts, axis=1)[None]
    sent_bias = jnp.moveaxis(local_bias.reshape(groups, NV, DK, column_parts, part_width), 3, 2)
    sent_bias = sent_bias.reshape(groups, item_count, DK, part_width)[None]
    got_maps = lax.all_to_all(sent_maps, "ctx", split_axis=2, concat_axis=0, tiled=True)
    got_bias = lax.all_to_all(sent_bias, "ctx", split_axis=2, concat_axis=0, tiled=True)

    def chain_step(state_now, incoming):
        return (chain_product(incoming[0], state_now) + incoming[1], state_now)

    _, entering_parts = lax.scan(
        chain_step, jnp.zeros(got_bias.shape[1:], jnp.float32), (got_maps, got_bias), unroll=4
    )
    returned_states = lax.all_to_all(
        entering_parts, "ctx", split_axis=0, concat_axis=2, tiled=True
    )
    entering = returned_states[0].reshape(groups, NV, column_parts, DK, part_width)
    entering = jnp.moveaxis(entering, 2, 3).reshape(groups, NV, DK, DV)
    if tie is not None:
        entering, tie = lax.optimization_barrier((entering, tie))
    _, outputs = lax.scan(block_apply, entering, parts)
    outputs = jnp.transpose(outputs, (1, 0, 3, 2, 4)).reshape(groups, positions, NV, DV)
    normed_out = rms_rows(outputs, gain_out).reshape(groups, positions, NV * DV)
    outcome = (section_input.astype(jnp.float32) + normed_out).astype(jnp.bfloat16)
    return outcome, tie


def solution(mesh):
    return jax.shard_map(
        local,
        mesh=mesh,
        in_specs=(
            P("dp", "ctx", None),
            P("section", "ctx", None),
            P("section", "ctx", None),
            P("section", None),
            P("section", None, None),
            P("section", None),
            P("section", None),
            P("section", None),
        ),
        out_specs=P(("dp", "section"), "ctx", None),
        check_vma=False,
    )
```
